256 devices in a mesh: exp: 64 (over y, z, core), grp: 4 (over x).
Axes of the slice: x: 4, y: 4, z: 8, core: 2. Of those that a mesh axis runs over, the one named last changes fastest.
Arguments:
- tiles: bfloat16 [1024, 256, 256], P(('exp', 'grp')), may hold values from -6 to 6
- tile_exposure: int32 [1024], P(('exp', 'grp')), may hold values from 0 to 511, as said below
- tile_patch: int32 [1024, 4], P(('exp', 'grp')), may hold values from 0 to 63, all different within a row; in each aligned block of 4 rows (0 to 3, 4 to 7, ...) at most 2 rows name the same one
- tile_offset: int32 [1024, 4, 2], P(('exp', 'grp')), may hold values from 0 to 256
- coeffs: bfloat16 [512, 10], P(('exp', 'grp')), may hold values from -2 to 2
- inv_var: bfloat16 [512], P(('exp', 'grp')), may hold values from 0.25 to 4
- vert_taps: bfloat16 [10, 41], replicated, may hold values from -1 to 1
- horiz_taps: bfloat16 [10, 41], replicated, may hold values from -1 to 1
Outputs:
- coadd: float32 [64, 512, 512], P('exp', 'grp')
The draws below stay inside these ranges and needn't reach their ends.
Inputs may be any that keep to these rules, and one draw needn't show every extreme that they name: `tile_exposure`: each exposure is named by exactly 1024 / 512 tiles. `tile_patch`: the entries of a row differ; among the rows of one device no patch is named by more than 2 rows. `tile_offset`: each tile lies wholly inside each patch listed for it.
All inputs are finite; a program needn't handle non-finite values.
Results may differ from the reference program's by a relative error of at most 0.0041.
Values may be sent and summed in bfloat16 or wider, within the bound.
No kernel may reach another device: no remote copies, remote signals or barrier semaphores. Data moves between devices by JAX's collectives and lax.ppermute only.
A program may use at most 128 MiB of HBM per device.

```python
import math
import jax
import jax.numpy as jnp
import numpy as np
from jax import lax

TS = 256
PS = 512
KW = 41
NB = 10
OVL = 4
TILE_DEV = 4
TILES = 1024
EXPOSURES = 512
PATCHES = 64
CAP = 2


def draw_tile_exposure(key, part):
    return (jax.random.permutation(key, TILES) % EXPOSURES).astype(jnp.int32)


def place_ends(result, rng, smallest, top_value):
    longest = result.shape.index(max(result.shape))
    spots = []
    for shift in (0, 1):
        where = [jax.random.randint(jax.random.fold_in(rng, axis), (), 0, length) for axis, length in enumerate(result.shape)]
        where[longest] = (where[longest] + shift) % result.shape[longest]
        spots.append(tuple(where))
    return result.at[spots[0]].set(smallest).at[spots[1]].set(top_value)


def level_of(own_key, dims, shards, least, top_value):
    def one(position, parts):
        draws = jax.random.uniform(jax.random.fold_in(jax.random.fold_in(own_key, 6), position), (parts,), jnp.float32, least / len(shards), top_value / len(shards))
        return jnp.repeat(jnp.exp(draws), dims[position] // parts).reshape((-1,) + (1,) * (len(dims) - position - 1))

    level = one(*shards[0])
    for cut in shards[1:]:
        level = level * one(*cut)
    return level


def deal_out(own_key, own, number, rows, number_of, top, limit, slope):
    ranking = jax.random.permutation(own_key, number_of)
    packed, common = portions_of(number_of, rows * top, limit, slope, True), portions_of(number_of, rows * top, limit, slope, False)
    places = jnp.arange(number_of)

    def named(sizes, offset_by):
        used = int((sizes > 0).sum())
        fixed = max(1, used // 4)
        moved = fixed + (places - fixed + offset_by * (used - fixed)) % max(1, number_of - fixed)
        return jnp.zeros((number_of,), jnp.int32).at[ranking[jnp.where(places < fixed, places, moved)]].set(jnp.asarray(sizes, jnp.int32))

    sizes = jnp.where(number % 4 == 0, named(packed, number // 4), named(common, number - number // 4 - 1))
    mixed = jax.random.permutation(jax.random.fold_in(own, 3), number_of)
    donor, sink = mixed[0:number_of // 2 * 2:2], mixed[1:number_of // 2 * 2:2]
    room = jnp.minimum(sizes[donor] - 1, limit - sizes[sink]) // 2
    room = jnp.where((donor == ranking[0]) | (sink == ranking[0]) | (sizes[sink] == 0), 0, jnp.maximum(room, 0))
    moved = jax.random.randint(jax.random.fold_in(own, 4), (number_of // 2,), 0, 1 << 20) % (room + 1)
    sizes = sizes.at[donor].add(-moved).at[sink].add(moved)
    members = jnp.searchsorted(jnp.cumsum(sizes), jnp.arange(rows * top), side="right").astype(jnp.int32)
    table = members.reshape(top, rows).T
    table = table[jax.random.permutation(jax.random.fold_in(own, 1), rows)]
    offset_by = jax.random.randint(jax.random.fold_in(own, 2), (rows, 1), 0, top)
    return jnp.take_along_axis(table, (jnp.arange(top)[None, :] + offset_by) % top, axis=1)


def portions_of(count, total, reach, skew, full):
    weights = [(1 << 20) // math.isqrt(standing ** skew) + 1 for standing in range(1, count + 1)]
    largest = reach if full else min(reach, max(-(-total // count), total * weights[0] // sum(weights)))
    least = 1 if total - largest >= count - 1 else 0
    given, surplus = [largest] + [least] * (count - 1), total - largest - least * (count - 1)
    while surplus > 0:
        movable = [i for i in range(1, count) if given[i] < largest] or [i for i in range(1, count) if given[i] < reach]
        pool, remaining = sum([weights[i] for i in movable]), surplus
        for i in movable:
            more = min(reach - given[i], max(1, remaining * weights[i] // pool), surplus)
            given[i] = given[i] + more
            surplus = surplus - more
    return np.array(given)


def scatter_about(key, extent, width, reach, split=(), held_as=jnp.bfloat16):
    factor_of = level_of(key, extent, split, -0.22, 0.18) if split else 1.0
    entries = jax.random.normal(key, extent, jnp.float32) * width * factor_of
    return jnp.minimum(jnp.maximum(entries, -reach), reach).astype(held_as)


def setup_inputs(seed: int = 0) -> dict:
    key_list = jax.random.split(jax.random.key(seed), 9)
    tiles = scatter_about(key_list[0], (TILES, TS, TS), 1.0, 6.0, ((0, 256),))
    tile_exposure = draw_tile_exposure(jax.random.fold_in(key_list[8], 71), 0)
    tile_patch_keys = jax.random.split(jax.random.fold_in(key_list[2], 1), TILES // TILE_DEV)
    tile_patch_turns = jax.random.permutation(jax.random.fold_in(key_list[2], 3), TILES // TILE_DEV)
    tile_patch = jax.vmap(lambda own, number: deal_out(jax.random.fold_in(key_list[2], 2), own, number, TILE_DEV, PATCHES, OVL, CAP, 2))(tile_patch_keys, tile_patch_turns).reshape((TILES, OVL))
    tile_offset = place_ends(jax.random.randint(key_list[3], (TILES, OVL, 2), 0, PS - TS + 1), jax.random.fold_in(key_list[3], 1), 0, PS - TS).astype(jnp.int32)
    coeffs = scatter_about(key_list[4], (EXPOSURES, NB), NB ** -0.5, 2.0, ((0, 256),))
    inv_var = jnp.clip(jnp.exp(math.log(4.0) - 2.7725887 * jax.random.uniform(key_list[5], (EXPOSURES,), jnp.float32) ** level_of(key_list[5], (EXPOSURES,), ((0, 256),), -0.2, 0.2)), 0.25, 4.0).astype(jnp.bfloat16)
    vert_taps = scatter_about(key_list[6], (NB, KW), KW ** -0.5, 1.0)
    horiz_taps = scatter_about(key_list[7], (NB, KW), KW ** -0.5, 1.0)
    return dict(tiles=tiles, tile_exposure=tile_exposure, tile_patch=tile_patch, tile_offset=tile_offset, coeffs=coeffs, inv_var=inv_var, vert_taps=vert_taps, horiz_taps=horiz_taps)


def band_matrix(filters, tile_side):
    terms, kernel_width = filters.shape
    half_width = (kernel_width - 1) // 2
    padding = tile_side - 1 - half_width
    padded = jnp.concatenate([jnp.zeros((terms, padding), jnp.float32), filters.astype(jnp.float32), jnp.zeros((terms, padding + 1), jnp.float32)], axis=1)
    tiled = jnp.tile(padded, (1, tile_side + 1))[:, : tile_side * (2 * tile_side + 1)]
    window = tiled.reshape(terms, tile_side, 2 * tile_side + 1)[:, :, :tile_side]
    return window[:, ::-1, :]


def reference(tiles, tile_exposure, tile_patch, tile_offset, coeffs, inv_var, vert_taps, horiz_taps):
    vband = band_matrix(vert_taps, TS)
    hband = band_matrix(horiz_taps, TS)
    coef_tile = coeffs[tile_exposure].astype(jnp.float32)
    weight_tile = inv_var[tile_exposure].astype(jnp.float32)
    groups = TILES // TILE_DEV
    block_tiles = tiles.reshape(groups, TILE_DEV, TS, TS)
    block_coef = coef_tile.reshape(groups, TILE_DEV, NB)
    block_weight = weight_tile.reshape(groups, TILE_DEV)
    block_patch = tile_patch.reshape(groups, TILE_DEV, OVL).astype(jnp.int32)
    block_offset = tile_offset.reshape(groups, TILE_DEV, OVL, 2).astype(jnp.int32)

    def one_block(carry, inputs):
        flux, cover = carry
        pixels, coef_rows, weights, patches, offsets = inputs
        rows_pass = jnp.einsum('tyk,bxk->tybx', pixels.astype(jnp.float32), hband, precision=lax.Precision.HIGHEST)
        partial_value = (rows_pass * coef_rows[:, None, :, None]).astype(jnp.bfloat16)
        smoothed = jnp.einsum('byk,tkbx->tyx', vband, partial_value.astype(jnp.float32), precision=lax.Precision.HIGHEST)
        weighted = (weights[:, None, None] * smoothed).astype(jnp.bfloat16)

        def add_entry(entry, inner):
            flux_in, cover_in = inner
            tile_pos = entry // OVL
            list_pos = entry % OVL
            patch = patches[tile_pos, list_pos].astype(jnp.int32)
            row_off = offsets[tile_pos, list_pos, 0].astype(jnp.int32)
            col_off = offsets[tile_pos, list_pos, 1].astype(jnp.int32)
            start = (patch, row_off, col_off)
            region = lax.dynamic_slice(flux_in, start, (1, TS, TS)) + weighted[tile_pos].astype(jnp.float32)[None]
            flux_in = lax.dynamic_update_slice(flux_in, region, start)
            spot = lax.dynamic_slice(cover_in, start, (1, TS, TS)) + weights[tile_pos]
            cover_in = lax.dynamic_update_slice(cover_in, spot, start)
            return (flux_in, cover_in)

        flux, cover = lax.fori_loop(0, TILE_DEV * OVL, add_entry, (flux, cover))
        return (flux, cover), None

    start_flux = jnp.zeros((PATCHES, PS, PS), jnp.float32)
    start_cover = jnp.zeros((PATCHES, PS, PS), jnp.float32)
    (flux, cover), _ = lax.scan(one_block, (start_flux, start_cover), (block_tiles, block_coef, block_weight, block_patch, block_offset))
    return flux / jnp.maximum(cover, 1.0)
```

```python
import jax
import jax.numpy as jnp
from jax import lax
from jax.sharding import PartitionSpec as P

PS = 512


def band_matrix(filters, tile_side):
    terms, kernel_width = filters.shape
    half_width = (kernel_width - 1) // 2
    row = lax.broadcasted_iota(jnp.int32, (kernel_width, tile_side, tile_side), 1)
    col = lax.broadcasted_iota(jnp.int32, (kernel_width, tile_side, tile_side), 2)
    tap = lax.broadcasted_iota(jnp.int32, (kernel_width, tile_side, tile_side), 0)
    onehot = (col - row + half_width == tap).astype(jnp.bfloat16)
    band = jnp.einsum("bd,dij->bij", filters, onehot, preferred_element_type=jnp.float32)
    return band.astype(jnp.bfloat16)


def per_device(
    tiles, tile_exposure, tile_patch, tile_offset, coeffs, inv_var, vert_taps, horiz_taps
):
    n_owners = lax.axis_size("exp")
    n_bands = lax.axis_size("grp")
    tile_count, tile_side, _ = tiles.shape
    listed = tile_patch.shape[1]
    terms = coeffs.shape[1]
    band_rows = PS // n_bands
    g = lax.axis_index("grp")

    packed = jnp.concatenate([coeffs, inv_var[:, None]], axis=1)
    packed = lax.all_gather(packed, "grp", axis=0, tiled=True)
    packed = lax.all_gather(packed, "exp", axis=0, tiled=True)

    vband = band_matrix(vert_taps, tile_side)
    hband = band_matrix(horiz_taps, tile_side)

    rows_pass = jnp.einsum("tyk,bxk->tybx", tiles, hband, preferred_element_type=jnp.float32)

    exposures = packed.shape[0]
    picker = (tile_exposure[:, None] == jnp.arange(exposures, dtype=jnp.int32)[None, :]).astype(
        jnp.bfloat16
    )
    picked = jnp.dot(picker, packed, preferred_element_type=jnp.float32)
    coef_tile = picked[:, :terms]
    weight_tile = picked[:, terms]

    partial_value = (rows_pass * coef_tile[:, None, :, None]).astype(jnp.bfloat16)
    smoothed = jnp.einsum(
        "byk,tkbx->tyx", vband, partial_value, preferred_element_type=jnp.float32
    )
    weighted = (weight_tile[:, None, None] * smoothed).astype(jnp.bfloat16)

    row_off = tile_offset[:, :, 0]
    col_off = tile_offset[:, :, 1]
    band_i = lax.broadcasted_iota(jnp.int32, (n_bands, tile_count, listed, band_rows, tile_side), 0)
    inner = lax.broadcasted_iota(jnp.int32, (n_bands, tile_count, listed, band_rows, tile_side), 3)
    src = lax.broadcasted_iota(jnp.int32, (n_bands, tile_count, listed, band_rows, tile_side), 4)
    picks = (src == band_i * band_rows + inner - row_off[None, :, :, None, None]).astype(
        jnp.bfloat16
    )
    slabs = jnp.einsum("gtjiy,tyx->gtjix", picks, weighted, preferred_element_type=jnp.float32)
    slabs = slabs.astype(jnp.bfloat16).reshape(n_bands * tile_count * listed, band_rows, tile_side)
    meta = jnp.stack(
        [
            tile_patch.astype(jnp.float32),
            row_off.astype(jnp.float32),
            col_off.astype(jnp.float32),
            jnp.broadcast_to(weight_tile[:, None], (tile_count, listed)),
        ],
        axis=-1,
    ).reshape(tile_count * listed, 4)
    meta_send = jnp.broadcast_to(meta[None], (n_bands,) + meta.shape).reshape(-1, 4)
    got_slabs = lax.all_to_all(slabs, "grp", split_axis=0, concat_axis=0, tiled=True)
    got_meta = lax.all_to_all(meta_send, "grp", split_axis=0, concat_axis=0, tiled=True)
    entries = got_meta.shape[0]
    got_patch = got_meta[:, 0].astype(jnp.int32)
    got_row = got_meta[:, 1].astype(jnp.int32)
    got_col = got_meta[:, 2].astype(jnp.int32)

    x_in = lax.broadcasted_iota(jnp.int32, (entries, tile_side, PS), 1)
    x_out = lax.broadcasted_iota(jnp.int32, (entries, tile_side, PS), 2)
    shifter = (x_out == got_col[:, None, None] + x_in).astype(jnp.bfloat16)
    shifted = jnp.einsum("kyx,kxX->kyX", got_slabs, shifter, preferred_element_type=jnp.float32)
    shifted = shifted.astype(jnp.bfloat16)
    owner_of = (
        got_patch[None, :] == jnp.arange(n_owners, dtype=jnp.int32)[:, None]
    ).astype(jnp.bfloat16)
    bands = jnp.einsum("pk,kyX->pyX", owner_of, shifted, preferred_element_type=jnp.float32)
    bands = bands.astype(jnp.bfloat16)

    per_owner = n_bands * 2
    onehot = (got_patch[:, None] == jnp.arange(n_owners, dtype=jnp.int32)[None, :]).astype(
        jnp.int32
    )
    before = jnp.cumsum(onehot, axis=0) - onehot
    rank = jnp.sum(before * onehot, axis=1)
    target = got_patch * per_owner + rank
    meta_slots = (
        jnp.zeros((n_owners * per_owner, 3), jnp.float32)
        .at[target]
        .set(got_meta[:, 1:], mode="drop")
    )

    recv_bands = lax.all_to_all(bands, "exp", split_axis=0, concat_axis=0, tiled=True)
    recv_meta = lax.all_to_all(meta_slots, "exp", split_axis=0, concat_axis=0, tiled=True)

    rows = recv_meta[:, 0].astype(jnp.int32)
    cols = recv_meta[:, 1].astype(jnp.int32)
    wts = recv_meta[:, 2]
    y_index = g * band_rows + jnp.arange(band_rows, dtype=jnp.int32)
    x_index = jnp.arange(PS, dtype=jnp.int32)
    row_mask = (
        (y_index[None, :] >= rows[:, None]) & (y_index[None, :] < rows[:, None] + tile_side)
    ).astype(jnp.float32) * wts[:, None]
    col_mask = (
        (x_index[None, :] >= cols[:, None]) & (x_index[None, :] < cols[:, None] + tile_side)
    ).astype(jnp.float32)
    cover = jnp.einsum("my,mx->yx", row_mask, col_mask, precision=lax.Precision.HIGHEST)
    flux = jnp.sum(recv_bands.astype(jnp.float32), axis=0)
    coadd = flux / jnp.maximum(cover, 1.0)
    return coadd[None]


def solution(mesh):
    in_specs = (
        P(("exp", "grp"), None, None),
        P(("exp", "grp")),
        P(("exp", "grp"), None),
        P(("exp", "grp"), None, None),
        P(("exp", "grp"), None),
        P(("exp", "grp")),
        P(),
        P(),
    )
    out_specs = P("exp", "grp", None)
    return jax.shard_map(
        per_device, mesh=mesh, in_specs=in_specs, out_specs=out_specs, check_vma=False
    )
```

```python
import jax
import jax.numpy as jnp
from jax import lax
from jax.sharding import PartitionSpec as P

PS = 512


def band_matrix(filters, tile_side):
    terms, kernel_width = filters.shape
    half_width = (kernel_width - 1) // 2
    row = lax.broadcasted_iota(jnp.int32, (kernel_width, tile_side, tile_side), 1)
    col = lax.broadcasted_iota(jnp.int32, (kernel_width, tile_side, tile_side), 2)
    tap = lax.broadcasted_iota(jnp.int32, (kernel_width, tile_side, tile_side), 0)
    onehot = (col - row + half_width == tap).astype(jnp.bfloat16)
    band = jnp.einsum("bd,dij->bij", filters, onehot, preferred_element_type=jnp.float32)
    return band.astype(jnp.bfloat16)


def per_device(
    tiles, tile_exposure, tile_patch, tile_offset, coeffs, inv_var, vert_taps, horiz_taps
):
    n_owners = lax.axis_size("exp")
    n_bands = lax.axis_size("grp")
    tile_count, tile_side, _ = tiles.shape
    listed = tile_patch.shape[1]
    terms = coeffs.shape[1]
    band_rows = PS // n_bands
    g = lax.axis_index("grp")

    packed = jnp.concatenate([coeffs, inv_var[:, None]], axis=1)
    packed = jnp.broadcast_to(packed[None], (n_bands,) + packed.shape)
    packed = lax.all_to_all(packed, "grp", split_axis=0, concat_axis=0, tiled=True)
    packed = packed.reshape(1, -1, terms + 1)
    packed = jnp.broadcast_to(packed, (n_owners,) + packed.shape[1:])
    packed = lax.all_to_all(packed, "exp", split_axis=0, concat_axis=0, tiled=True)
    packed = packed.reshape(-1, terms + 1)

    vband = band_matrix(vert_taps, tile_side)
    hband = band_matrix(horiz_taps, tile_side)

    rows_pass = jnp.einsum("tyk,bxk->tybx", tiles, hband, preferred_element_type=jnp.float32)

    exposures = packed.shape[0]
    picker = (tile_exposure[:, None] == jnp.arange(exposures, dtype=jnp.int32)[None, :]).astype(
        jnp.bfloat16
    )
    picked = jnp.dot(picker, packed, preferred_element_type=jnp.float32)
    coef_tile = picked[:, :terms]
    weight_tile = picked[:, terms]

    partial_value = (rows_pass * coef_tile[:, None, :, None]).astype(jnp.bfloat16)
    smoothed = jnp.einsum(
        "byk,tkbx->tyx", vband, partial_value, preferred_element_type=jnp.float32
    )
    weighted = (weight_tile[:, None, None] * smoothed).astype(jnp.bfloat16)

    row_off = tile_offset[:, :, 0]
    col_off = tile_offset[:, :, 1]
    band_i = lax.broadcasted_iota(jnp.int32, (n_bands, tile_count, listed, band_rows, tile_side), 0)
    inner = lax.broadcasted_iota(jnp.int32, (n_bands, tile_count, listed, band_rows, tile_side), 3)
    src = lax.broadcasted_iota(jnp.int32, (n_bands, tile_count, listed, band_rows, tile_side), 4)
    picks = (src == band_i * band_rows + inner - row_off[None, :, :, None, None]).astype(
        jnp.bfloat16
    )
    slabs = jnp.einsum("gtjiy,tyx->gtjix", picks, weighted, preferred_element_type=jnp.float32)
    slabs = slabs.astype(jnp.bfloat16).reshape(n_bands * tile_count * listed, band_rows, tile_side)
    meta = jnp.stack(
        [
            tile_patch.astype(jnp.float32),
            row_off.astype(jnp.float32),
            col_off.astype(jnp.float32),
            jnp.broadcast_to(weight_tile[:, None], (tile_count, listed)),
        ],
        axis=-1,
    ).reshape(tile_count * listed, 4)
    meta_send = jnp.broadcast_to(meta[None], (n_bands,) + meta.shape).reshape(-1, 4)
    got_slabs = lax.all_to_all(slabs, "grp", split_axis=0, concat_axis=0, tiled=True)
    got_meta = lax.all_to_all(meta_send, "grp", split_axis=0, concat_axis=0, tiled=True)
    entries = got_meta.shape[0]
    got_patch = got_meta[:, 0].astype(jnp.int32)
    got_row = got_meta[:, 1].astype(jnp.int32)
    got_col = got_meta[:, 2].astype(jnp.int32)

    x_in = lax.broadcasted_iota(jnp.int32, (entries, tile_side, PS), 1)
    x_out = lax.broadcasted_iota(jnp.int32, (entries, tile_side, PS), 2)
    shifter = (x_out == got_col[:, None, None] + x_in).astype(jnp.bfloat16)
    shifted = jnp.einsum("kyx,kxX->kyX", got_slabs, shifter, preferred_element_type=jnp.float32)
    shifted = shifted.astype(jnp.bfloat16)
    owner_of = (
        got_patch[None, :] == jnp.arange(n_owners, dtype=jnp.int32)[:, None]
    ).astype(jnp.bfloat16)
    bands = jnp.einsum("pk,kyX->pyX", owner_of, shifted, preferred_element_type=jnp.float32)

    per_owner = n_bands * 2
    onehot = (got_patch[:, None] == jnp.arange(n_owners, dtype=jnp.int32)[None, :]).astype(
        jnp.int32
    )
    before = jnp.cumsum(onehot, axis=0) - onehot
    rank = jnp.sum(before * onehot, axis=1)
    target = got_patch * per_owner + rank
    meta_slots = (
        jnp.zeros((n_owners * per_owner, 3), jnp.float32)
        .at[target]
        .set(got_meta[:, 1:], mode="drop")
    )

    flux = lax.psum_scatter(bands, "exp", scatter_dimension=0, tiled=True)[0]
    recv_meta = lax.all_to_all(meta_slots, "exp", split_axis=0, concat_axis=0, tiled=True)

    rows = recv_meta[:, 0].astype(jnp.int32)
    cols = recv_meta[:, 1].astype(jnp.int32)
    wts = recv_meta[:, 2]
    y_index = g * band_rows + jnp.arange(band_rows, dtype=jnp.int32)
    x_index = jnp.arange(PS, dtype=jnp.int32)
    row_mask = (
        (y_index[None, :] >= rows[:, None]) & (y_index[None, :] < rows[:, None] + tile_side)
    ).astype(jnp.float32) * wts[:, None]
    col_mask = (
        (x_index[None, :] >= cols[:, None]) & (x_index[None, :] < cols[:, None] + tile_side)
    ).astype(jnp.float32)
    cover = jnp.einsum("my,mx->yx", row_mask, col_mask, precision=lax.Precision.HIGHEST)
    coadd = flux / jnp.maximum(cover, 1.0)
    return coadd[None]


def solution(mesh):
    in_specs = (
        P(("exp", "grp"), None, None),
        P(("exp", "grp")),
        P(("exp", "grp"), None),
        P(("exp", "grp"), None, None),
        P(("exp", "grp"), None),
        P(("exp", "grp")),
        P(),
        P(),
    )
    out_specs = P("exp", "grp", None)
    return jax.shard_map(
        per_device, mesh=mesh, in_specs=in_specs, out_specs=out_specs, check_vma=False
    )
```

```python
import jax
import jax.numpy as jnp
from jax import lax
from jax.sharding import Mesh
from jax.sharding import PartitionSpec as P

PS = 512
EXP = ("ey", "ez", "ec")
CHIP = ("ey", "ez")
PAIR = ("ec", "grp")


def band_matrix(filters, tile_side):
    terms, kernel_width = filters.shape
    half_width = (kernel_width - 1) // 2
    row = lax.broadcasted_iota(jnp.int32, (kernel_width, tile_side, tile_side), 1)
    col = lax.broadcasted_iota(jnp.int32, (kernel_width, tile_side, tile_side), 2)
    tap = lax.broadcasted_iota(jnp.int32, (kernel_width, tile_side, tile_side), 0)
    onehot = (col - row + half_width == tap).astype(jnp.bfloat16)
    band = jnp.einsum("bd,dij->bij", filters, onehot, preferred_element_type=jnp.float32)
    return band.astype(jnp.bfloat16)


def per_device(
    tiles, tile_exposure, tile_patch, tile_offset, coeffs, inv_var, vert_taps, horiz_taps
):
    n_owners = lax.axis_size(EXP)
    n_bands = lax.axis_size("grp")
    tile_count, tile_side, _ = tiles.shape
    listed = tile_patch.shape[1]
    terms = coeffs.shape[1]
    band_rows = PS // n_bands
    g = lax.axis_index("grp")
    h = lax.axis_index("ec")
    n_halves = lax.axis_size("ec")

    packed = jnp.concatenate([coeffs, inv_var[:, None]], axis=1)
    packed = jnp.broadcast_to(packed[None], (n_bands,) + packed.shape)
    packed = lax.all_to_all(packed, "grp", split_axis=0, concat_axis=0, tiled=True)
    packed = packed.reshape(1, -1, terms + 1)
    packed = jnp.broadcast_to(packed, (n_owners,) + packed.shape[1:])
    packed = lax.all_to_all(packed, EXP, split_axis=0, concat_axis=0, tiled=True)
    packed = packed.reshape(-1, terms + 1)

    vband = band_matrix(vert_taps, tile_side)
    hband = band_matrix(horiz_taps, tile_side)

    rows_pass = jnp.einsum("tyk,bxk->tybx", tiles, hband, preferred_element_type=jnp.float32)

    exposures = packed.shape[0]
    picker = (tile_exposure[:, None] == jnp.arange(exposures, dtype=jnp.int32)[None, :]).astype(
        jnp.bfloat16
    )
    picked = jnp.dot(picker, packed, preferred_element_type=jnp.float32)
    coef_tile = picked[:, :terms]
    weight_tile = picked[:, terms]

    partial_value = (rows_pass * coef_tile[:, None, :, None]).astype(jnp.bfloat16)
    smoothed = jnp.einsum(
        "byk,tkbx->tyx", vband, partial_value, preferred_element_type=jnp.float32
    )
    weighted = (weight_tile[:, None, None] * smoothed).astype(jnp.bfloat16)

    peers = n_bands * n_halves
    piece_rows = band_rows // n_halves
    row_off = tile_offset[:, :, 0]
    col_off = tile_offset[:, :, 1]
    shape5 = (peers, tile_count, listed, piece_rows, tile_side)
    dest = lax.broadcasted_iota(jnp.int32, shape5, 0)
    inner = lax.broadcasted_iota(jnp.int32, shape5, 3)
    src = lax.broadcasted_iota(jnp.int32, shape5, 4)
    first_row = (dest % n_bands) * band_rows + (dest // n_bands) * piece_rows
    picks = (src == first_row + inner - row_off[None, :, :, None, None]).astype(jnp.bfloat16)
    slabs = jnp.einsum("dtjiy,tyx->dtjix", picks, weighted, preferred_element_type=jnp.float32)
    slabs = slabs.astype(jnp.bfloat16).reshape(peers * tile_count * listed, piece_rows, tile_side)
    meta = jnp.stack(
        [
            tile_patch.astype(jnp.float32),
            row_off.astype(jnp.float32),
            col_off.astype(jnp.float32),
            jnp.broadcast_to(weight_tile[:, None], (tile_count, listed)),
        ],
        axis=-1,
    ).reshape(tile_count * listed, 4)
    meta_send = jnp.broadcast_to(meta[None], (peers,) + meta.shape).reshape(-1, 4)
    got_slabs = lax.all_to_all(slabs, PAIR, split_axis=0, concat_axis=0, tiled=True)
    got_meta = lax.all_to_all(meta_send, PAIR, split_axis=0, concat_axis=0, tiled=True)
    entries = got_meta.shape[0]
    got_patch = got_meta[:, 0].astype(jnp.int32)
    got_col = got_meta[:, 2].astype(jnp.int32)

    x_in = lax.broadcasted_iota(jnp.int32, (entries, tile_side, PS), 1)
    x_out = lax.broadcasted_iota(jnp.int32, (entries, tile_side, PS), 2)
    shifter = (x_out == got_col[:, None, None] + x_in).astype(jnp.bfloat16)
    shifted = jnp.einsum("kyx,kxX->kyX", got_slabs, shifter, preferred_element_type=jnp.float32)
    shifted = shifted.astype(jnp.bfloat16)
    owner_of = (
        got_patch[None, :] == jnp.arange(n_owners, dtype=jnp.int32)[:, None]
    ).astype(jnp.bfloat16)
    pieces = jnp.einsum("pk,kyX->pyX", owner_of, shifted, preferred_element_type=jnp.float32)

    per_owner = peers * 2
    onehot = (got_patch[:, None] == jnp.arange(n_owners, dtype=jnp.int32)[None, :]).astype(
        jnp.int32
    )
    before = jnp.cumsum(onehot, axis=0) - onehot
    rank = jnp.sum(before * onehot, axis=1)
    target = got_patch * per_owner + rank
    keep = (h == 0).astype(jnp.float32)
    meta_cover = jnp.concatenate([got_meta[:, 1:3], got_meta[:, 3:4] * keep], axis=1)
    meta_slots = (
        jnp.zeros((n_owners * per_owner, 3), jnp.float32)
        .at[target]
        .set(meta_cover, mode="drop")
    )

    chips = n_owners // n_halves
    pieces = pieces.reshape(chips, n_halves, piece_rows, PS)
    mine = lax.psum_scatter(pieces, CHIP, scatter_dimension=0, tiled=True)[0]
    other = lax.ppermute(
        jnp.where(h == 0, mine[1], mine[0]), "ec", perm=[(0, 1), (1, 0)]
    )
    own_half = jnp.where(h == 0, mine[0], mine[1])
    flux = jnp.where(
        h == 0,
        jnp.concatenate([own_half, other], axis=0),
        jnp.concatenate([other, own_half], axis=0),
    )
    recv_meta = lax.all_to_all(meta_slots, EXP, split_axis=0, concat_axis=0, tiled=True)

    rows = recv_meta[:, 0].astype(jnp.int32)
    cols = recv_meta[:, 1].astype(jnp.int32)
    wts = recv_meta[:, 2]
    y_index = g * band_rows + jnp.arange(band_rows, dtype=jnp.int32)
    x_index = jnp.arange(PS, dtype=jnp.int32)
    row_mask = (
        (y_index[None, :] >= rows[:, None]) & (y_index[None, :] < rows[:, None] + tile_side)
    ).astype(jnp.float32) * wts[:, None]
    col_mask = (
        (x_index[None, :] >= cols[:, None]) & (x_index[None, :] < cols[:, None] + tile_side)
    ).astype(jnp.float32)
    cover = jnp.einsum("my,mx->yx", row_mask, col_mask, precision=lax.Precision.HIGHEST)
    coadd = flux / jnp.maximum(cover, 1.0)
    return coadd[None]


def solution(mesh):
    n_exp, n_grp = mesh.devices.shape
    n_core = 2
    n_y = 4
    split = Mesh(mesh.devices.reshape(n_y, n_exp // (n_y * n_core), n_core, n_grp), EXP + ("grp",))
    every = EXP + ("grp",)
    in_specs = (
        P(every, None, None),
        P(every),
        P(every, None),
        P(every, None, None),
        P(every, None),
        P(every),
        P(),
        P(),
    )
    out_specs = P(EXP, "grp", None)
    return jax.shard_map(
        per_device, mesh=split, in_specs=in_specs, out_specs=out_specs, check_vma=False
    )
```

```python
import jax
import jax.numpy as jnp
from jax import lax
from jax.sharding import PartitionSpec as P

PS = 512


def band_matrix(filters, tile_side):
    terms, kernel_width = filters.shape
    half_width = (kernel_width - 1) // 2
    row = lax.broadcasted_iota(jnp.int32, (kernel_width, tile_side, tile_side), 1)
    col = lax.broadcasted_iota(jnp.int32, (kernel_width, tile_side, tile_side), 2)
    tap = lax.broadcasted_iota(jnp.int32, (kernel_width, tile_side, tile_side), 0)
    onehot = (col - row + half_width == tap).astype(jnp.bfloat16)
    band = jnp.einsum("bd,dij->bij", filters, onehot, preferred_element_type=jnp.float32)
    return band.astype(jnp.bfloat16)


def per_device(
    tiles, tile_exposure, tile_patch, tile_offset, coeffs, inv_var, vert_taps, horiz_taps
):
    n_owners = lax.axis_size("exp")
    n_bands = lax.axis_size("grp")
    tile_count, tile_side, _ = tiles.shape
    listed = tile_patch.shape[1]
    terms = coeffs.shape[1]
    band_rows = PS // n_bands
    g = lax.axis_index("grp")

    packed = jnp.concatenate([coeffs, inv_var[:, None]], axis=1)
    packed = jnp.broadcast_to(packed[None], (n_bands,) + packed.shape)
    packed = lax.all_to_all(packed, "grp", split_axis=0, concat_axis=0, tiled=True)
    packed = packed.reshape(1, -1, terms + 1)
    packed = jnp.broadcast_to(packed, (n_owners,) + packed.shape[1:])
    packed = lax.all_to_all(packed, "exp", split_axis=0, concat_axis=0, tiled=True)
    packed = packed.reshape(-1, terms + 1)

    vband = band_matrix(vert_taps, tile_side)
    hband = band_matrix(horiz_taps, tile_side)

    rows_pass = jnp.einsum("tyk,bxk->tybx", tiles, hband, preferred_element_type=jnp.float32)

    exposures = packed.shape[0]
    picker = (tile_exposure[:, None] == jnp.arange(exposures, dtype=jnp.int32)[None, :]).astype(
        jnp.bfloat16
    )
    picked = jnp.dot(picker, packed, preferred_element_type=jnp.float32)
    coef_tile = picked[:, :terms]
    weight_tile = picked[:, terms]

    partial_value = (rows_pass * coef_tile[:, None, :, None]).astype(jnp.bfloat16)
    smoothed = jnp.einsum(
        "byk,tkbx->tyx", vband, partial_value, preferred_element_type=jnp.float32
    )
    weighted = (weight_tile[:, None, None] * smoothed).astype(jnp.bfloat16)

    n_chunks = 2
    chunk_rows = band_rows // n_chunks
    row_off = tile_offset[:, :, 0]
    col_off = tile_offset[:, :, 1]
    meta = jnp.stack(
        [
            tile_patch.astype(jnp.float32),
            row_off.astype(jnp.float32),
            col_off.astype(jnp.float32),
            jnp.broadcast_to(weight_tile[:, None], (tile_count, listed)),
        ],
        axis=-1,
    ).reshape(tile_count * listed, 4)
    meta_send = jnp.broadcast_to(meta[None], (n_bands,) + meta.shape).reshape(-1, 4)
    got_meta = lax.all_to_all(meta_send, "grp", split_axis=0, concat_axis=0, tiled=True)
    entries = got_meta.shape[0]
    got_patch = got_meta[:, 0].astype(jnp.int32)
    got_col = got_meta[:, 2].astype(jnp.int32)
    owner_of = (
        got_patch[None, :] == jnp.arange(n_owners, dtype=jnp.int32)[:, None]
    ).astype(jnp.bfloat16)
    x_in = lax.broadcasted_iota(jnp.int32, (entries, tile_side, PS), 1)
    x_out = lax.broadcasted_iota(jnp.int32, (entries, tile_side, PS), 2)
    shifter = (x_out == got_col[:, None, None] + x_in).astype(jnp.bfloat16)

    flat_weighted = weighted.reshape(tile_count * tile_side, tile_side)
    shape6 = (n_bands, tile_count, listed, chunk_rows, tile_count, tile_side)
    band_i = lax.broadcasted_iota(jnp.int32, shape6, 0)
    tile_i = lax.broadcasted_iota(jnp.int32, shape6, 1)
    inner = lax.broadcasted_iota(jnp.int32, shape6, 3)
    tile_k = lax.broadcasted_iota(jnp.int32, shape6, 4)
    src = lax.broadcasted_iota(jnp.int32, shape6, 5)
    flux_chunks = []
    for c in range(n_chunks):
        first = band_i * band_rows + c * chunk_rows + inner
        picks = (
            (tile_i == tile_k) & (src == first - row_off[None, :, :, None, None, None])
        ).astype(jnp.bfloat16)
        picks = picks.reshape(n_bands * tile_count * listed * chunk_rows, tile_count * tile_side)
        slabs = jnp.dot(picks, flat_weighted, preferred_element_type=jnp.float32)
        slabs = slabs.astype(jnp.bfloat16).reshape(
            n_bands * tile_count * listed, chunk_rows, tile_side
        )
        got_slabs = lax.all_to_all(slabs, "grp", split_axis=0, concat_axis=0, tiled=True)
        shifted = jnp.einsum(
            "kyx,kxX->kyX", got_slabs, shifter, preferred_element_type=jnp.float32
        ).astype(jnp.bfloat16)
        bands = jnp.dot(
            owner_of, shifted.reshape(entries, chunk_rows * PS), preferred_element_type=jnp.float32
        ).reshape(n_owners, chunk_rows, PS)
        flux_chunks.append(lax.psum_scatter(bands, "exp", scatter_dimension=0, tiled=True)[0])
    flux = jnp.concatenate(flux_chunks, axis=0)

    per_owner = n_bands * 2
    onehot = (got_patch[:, None] == jnp.arange(n_owners, dtype=jnp.int32)[None, :]).astype(
        jnp.int32
    )
    before = jnp.cumsum(onehot, axis=0) - onehot
    rank = jnp.sum(before * onehot, axis=1)
    target = got_patch * per_owner + rank
    meta_slots = (
        jnp.zeros((n_owners * per_owner, 3), jnp.float32)
        .at[target]
        .set(got_meta[:, 1:], mode="drop")
    )
    recv_meta = lax.all_to_all(meta_slots, "exp", split_axis=0, concat_axis=0, tiled=True)

    rows = recv_meta[:, 0].astype(jnp.int32)
    cols = recv_meta[:, 1].astype(jnp.int32)
    wts = recv_meta[:, 2]
    y_index = g * band_rows + jnp.arange(band_rows, dtype=jnp.int32)
    x_index = jnp.arange(PS, dtype=jnp.int32)
    row_mask = (
        (y_index[None, :] >= rows[:, None]) & (y_index[None, :] < rows[:, None] + tile_side)
    ).astype(jnp.float32) * wts[:, None]
    col_mask = (
        (x_index[None, :] >= cols[:, None]) & (x_index[None, :] < cols[:, None] + tile_side)
    ).astype(jnp.float32)
    cover = jnp.einsum("my,mx->yx", row_mask, col_mask, precision=lax.Precision.HIGHEST)
    coadd = flux / jnp.maximum(cover, 1.0)
    return coadd[None]


def solution(mesh):
    in_specs = (
        P(("exp", "grp"), None, None),
        P(("exp", "grp")),
        P(("exp", "grp"), None),
        P(("exp", "grp"), None, None),
        P(("exp", "grp"), None),
        P(("exp", "grp")),
        P(),
        P(),
    )
    out_specs = P("exp", "grp", None)
    return jax.shard_map(
        per_device, mesh=mesh, in_specs=in_specs, out_specs=out_specs, check_vma=False
    )
```

```python
import jax
import jax.numpy as jnp
from jax import lax
from jax.sharding import Mesh
from jax.sharding import PartitionSpec as P

PS = 512
EXP = ("ey", "ez", "ec")
CHIP = ("ey", "ez")


def band_matrix(filters, tile_side):
    terms, kernel_width = filters.shape
    half_width = (kernel_width - 1) // 2
    row = lax.broadcasted_iota(jnp.int32, (kernel_width, tile_side, tile_side), 1)
    col = lax.broadcasted_iota(jnp.int32, (kernel_width, tile_side, tile_side), 2)
    tap = lax.broadcasted_iota(jnp.int32, (kernel_width, tile_side, tile_side), 0)
    onehot = (col - row + half_width == tap).astype(jnp.bfloat16)
    band = jnp.einsum("bd,dij->bij", filters, onehot, preferred_element_type=jnp.float32)
    return band.astype(jnp.bfloat16)


def per_device(
    tiles, tile_exposure, tile_patch, tile_offset, coeffs, inv_var, vert_taps, horiz_taps
):
    n_owners = lax.axis_size(EXP)
    n_bands = lax.axis_size("grp")
    tile_count, tile_side, _ = tiles.shape
    listed = tile_patch.shape[1]
    terms = coeffs.shape[1]
    band_rows = PS // n_bands
    g = lax.axis_index("grp")
    h = lax.axis_index("ec")
    n_halves = lax.axis_size("ec")

    packed = jnp.concatenate([coeffs, inv_var[:, None]], axis=1)
    packed = jnp.broadcast_to(packed[None], (n_bands,) + packed.shape)
    packed = lax.all_to_all(packed, "grp", split_axis=0, concat_axis=0, tiled=True)
    packed = packed.reshape(1, -1, terms + 1)
    packed = jnp.broadcast_to(packed, (n_owners,) + packed.shape[1:])
    packed = lax.all_to_all(packed, EXP, split_axis=0, concat_axis=0, tiled=True)
    packed = packed.reshape(-1, terms + 1)

    vband = band_matrix(vert_taps, tile_side)
    hband = band_matrix(horiz_taps, tile_side)

    rows_pass = jnp.einsum("tyk,bxk->tybx", tiles, hband, preferred_element_type=jnp.float32)

    exposures = packed.shape[0]
    picker = (tile_exposure[:, None] == jnp.arange(exposures, dtype=jnp.int32)[None, :]).astype(
        jnp.bfloat16
    )
    picked = jnp.dot(picker, packed, preferred_element_type=jnp.float32)
    coef_tile = picked[:, :terms]
    weight_tile = picked[:, terms]

    partial_value = (rows_pass * coef_tile[:, None, :, None]).astype(jnp.bfloat16)
    smoothed = jnp.einsum(
        "byk,tkbx->tyx", vband, partial_value, preferred_element_type=jnp.float32
    )
    weighted = (weight_tile[:, None, None] * smoothed).astype(jnp.bfloat16)

    row_off = tile_offset[:, :, 0]
    col_off = tile_offset[:, :, 1]
    band_i = lax.broadcasted_iota(jnp.int32, (n_bands, tile_count, listed, band_rows, tile_side), 0)
    inner = lax.broadcasted_iota(jnp.int32, (n_bands, tile_count, listed, band_rows, tile_side), 3)
    src = lax.broadcasted_iota(jnp.int32, (n_bands, tile_count, listed, band_rows, tile_side), 4)
    picks = (src == band_i * band_rows + inner - row_off[None, :, :, None, None]).astype(
        jnp.bfloat16
    )
    slabs = jnp.einsum("gtjiy,tyx->gtjix", picks, weighted, preferred_element_type=jnp.float32)
    slabs = slabs.astype(jnp.bfloat16).reshape(n_bands * tile_count * listed, band_rows, tile_side)
    meta = jnp.stack(
        [
            tile_patch.astype(jnp.float32),
            row_off.astype(jnp.float32),
            col_off.astype(jnp.float32),
            jnp.broadcast_to(weight_tile[:, None], (tile_count, listed)),
        ],
        axis=-1,
    ).reshape(tile_count * listed, 4)
    meta_send = jnp.broadcast_to(meta[None], (n_bands,) + meta.shape).reshape(-1, 4)
    got_slabs = lax.all_to_all(slabs, "grp", split_axis=0, concat_axis=0, tiled=True)
    got_meta = lax.all_to_all(meta_send, "grp", split_axis=0, concat_axis=0, tiled=True)
    entries = got_meta.shape[0]
    got_patch = got_meta[:, 0].astype(jnp.int32)
    got_row = got_meta[:, 1].astype(jnp.int32)
    got_col = got_meta[:, 2].astype(jnp.int32)

    x_in = lax.broadcasted_iota(jnp.int32, (entries, tile_side, PS), 1)
    x_out = lax.broadcasted_iota(jnp.int32, (entries, tile_side, PS), 2)
    shifter = (x_out == got_col[:, None, None] + x_in).astype(jnp.bfloat16)
    shifted = jnp.einsum("kyx,kxX->kyX", got_slabs, shifter, preferred_element_type=jnp.float32)
    shifted = shifted.astype(jnp.bfloat16)
    owner_of = (
        got_patch[None, :] == jnp.arange(n_owners, dtype=jnp.int32)[:, None]
    ).astype(jnp.bfloat16)
    bands = jnp.dot(
        owner_of, shifted.reshape(entries, band_rows * PS), preferred_element_type=jnp.float32
    ).reshape(n_owners // n_halves, n_halves, band_rows, PS)

    per_owner = n_bands * 2
    onehot = (got_patch[:, None] == jnp.arange(n_owners, dtype=jnp.int32)[None, :]).astype(
        jnp.int32
    )
    before = jnp.cumsum(onehot, axis=0) - onehot
    rank = jnp.sum(before * onehot, axis=1)
    target = got_patch * per_owner + rank
    meta_slots = (
        jnp.zeros((n_owners * per_owner, 3), jnp.float32)
        .at[target]
        .set(got_meta[:, 1:], mode="drop")
    )

    keep = lax.dynamic_index_in_dim(bands, h, axis=1, keepdims=False)
    give = lax.dynamic_index_in_dim(bands, 1 - h, axis=1, keepdims=False)
    pair = keep + lax.ppermute(give, "ec", perm=[(0, 1), (1, 0)])
    recv_bands = lax.all_to_all(pair.astype(jnp.bfloat16), CHIP, split_axis=0, concat_axis=0, tiled=True)
    flux = jnp.sum(recv_bands.astype(jnp.float32), axis=0)
    recv_meta = lax.all_to_all(meta_slots, EXP, split_axis=0, concat_axis=0, tiled=True)

    rows = recv_meta[:, 0].astype(jnp.int32)
    cols = recv_meta[:, 1].astype(jnp.int32)
    wts = recv_meta[:, 2]
    y_index = g * band_rows + jnp.arange(band_rows, dtype=jnp.int32)
    x_index = jnp.arange(PS, dtype=jnp.int32)
    row_mask = (
        (y_index[None, :] >= rows[:, None]) & (y_index[None, :] < rows[:, None] + tile_side)
    ).astype(jnp.float32) * wts[:, None]
    col_mask = (
        (x_index[None, :] >= cols[:, None]) & (x_index[None, :] < cols[:, None] + tile_side)
    ).astype(jnp.float32)
    cover = jnp.einsum("my,mx->yx", row_mask, col_mask, precision=lax.Precision.HIGHEST)
    coadd = flux / jnp.maximum(cover, 1.0)
    return coadd[None]


def solution(mesh):
    n_exp, n_grp = mesh.devices.shape
    n_core = 2
    n_y = 4
    split = Mesh(mesh.devices.reshape(n_y, n_exp // (n_y * n_core), n_core, n_grp), EXP + ("grp",))
    every = EXP + ("grp",)
    in_specs = (
        P(every, None, None),
        P(every),
        P(every, None),
        P(every, None, None),
        P(every, None),
        P(every),
        P(),
        P(),
    )
    out_specs = P(EXP, "grp", None)
    return jax.shard_map(
        per_device, mesh=split, in_specs=in_specs, out_specs=out_specs, check_vma=False
    )
```

```python
import jax
import jax.numpy as jnp
from jax import lax
from jax.sharding import Mesh
from jax.sharding import PartitionSpec as P

PS = 512
EXP = ("ey", "ez", "ec")
CHIP = ("ey", "ez")


def band_matrix(filters, tile_side):
    terms, kernel_width = filters.shape
    half_width = (kernel_width - 1) // 2
    row = lax.broadcasted_iota(jnp.int32, (kernel_width, tile_side, tile_side), 1)
    col = lax.broadcasted_iota(jnp.int32, (kernel_width, tile_side, tile_side), 2)
    tap = lax.broadcasted_iota(jnp.int32, (kernel_width, tile_side, tile_side), 0)
    onehot = (col - row + half_width == tap).astype(jnp.bfloat16)
    band = jnp.einsum("bd,dij->bij", filters, onehot, preferred_element_type=jnp.float32)
    return band.astype(jnp.bfloat16)


def per_device(
    tiles, tile_exposure, tile_patch, tile_offset, coeffs, inv_var, vert_taps, horiz_taps
):
    n_owners = lax.axis_size(EXP)
    n_bands = lax.axis_size("grp")
    tile_count, tile_side, _ = tiles.shape
    listed = tile_patch.shape[1]
    terms = coeffs.shape[1]
    band_rows = PS // n_bands
    g = lax.axis_index("grp")
    h = lax.axis_index("ec")
    n_halves = lax.axis_size("ec")

    packed = jnp.concatenate([coeffs, inv_var[:, None]], axis=1)
    packed = jnp.broadcast_to(packed[None], (n_bands,) + packed.shape)
    packed = lax.all_to_all(packed, "grp", split_axis=0, concat_axis=0, tiled=True)
    packed = packed.reshape(1, 1, -1)
    packed = jnp.broadcast_to(packed, (n_owners,) + packed.shape[1:])
    packed = lax.all_to_all(packed, EXP, split_axis=0, concat_axis=0, tiled=True)
    packed = packed.reshape(-1, terms + 1)

    vband = band_matrix(vert_taps, tile_side)
    hband = band_matrix(horiz_taps, tile_side)

    rows_pass = jnp.einsum("tyk,bxk->tybx", tiles, hband, preferred_element_type=jnp.float32)

    exposures = packed.shape[0]
    picker = (tile_exposure[:, None] == jnp.arange(exposures, dtype=jnp.int32)[None, :]).astype(
        jnp.bfloat16
    )
    picked = jnp.dot(picker, packed, preferred_element_type=jnp.float32)
    coef_tile = picked[:, :terms]
    weight_tile = picked[:, terms]

    partial_value = (rows_pass * coef_tile[:, None, :, None]).astype(jnp.bfloat16)
    smoothed = jnp.einsum(
        "byk,tkbx->tyx", vband, partial_value, preferred_element_type=jnp.float32
    )
    weighted = (weight_tile[:, None, None] * smoothed).astype(jnp.bfloat16)

    row_off = tile_offset[:, :, 0]
    col_off = tile_offset[:, :, 1]
    band_i = lax.broadcasted_iota(jnp.int32, (n_bands, tile_count, listed, band_rows, tile_side), 0)
    inner = lax.broadcasted_iota(jnp.int32, (n_bands, tile_count, listed, band_rows, tile_side), 3)
    src = lax.broadcasted_iota(jnp.int32, (n_bands, tile_count, listed, band_rows, tile_side), 4)
    picks = (src == band_i * band_rows + inner - row_off[None, :, :, None, None]).astype(
        jnp.bfloat16
    )
    slabs = jnp.einsum("gtjiy,tyx->gtjix", picks, weighted, preferred_element_type=jnp.float32)
    slabs = slabs.astype(jnp.bfloat16).reshape(n_bands * tile_count * listed, band_rows, tile_side)
    meta = jnp.stack(
        [
            tile_patch.astype(jnp.float32),
            row_off.astype(jnp.float32),
            col_off.astype(jnp.float32),
            jnp.broadcast_to(weight_tile[:, None], (tile_count, listed)),
        ],
        axis=-1,
    ).reshape(tile_count * listed, 4)
    meta_send = jnp.broadcast_to(meta[None], (n_bands,) + meta.shape).reshape(-1, 4)
    got_slabs = lax.all_to_all(slabs, "grp", split_axis=0, concat_axis=0, tiled=True)
    got_meta = lax.all_to_all(meta_send, "grp", split_axis=0, concat_axis=0, tiled=True)
    entries = got_meta.shape[0]
    got_patch = got_meta[:, 0].astype(jnp.int32)
    got_row = got_meta[:, 1].astype(jnp.int32)
    got_col = got_meta[:, 2].astype(jnp.int32)

    x_in = lax.broadcasted_iota(jnp.int32, (entries, tile_side, PS), 1)
    x_out = lax.broadcasted_iota(jnp.int32, (entries, tile_side, PS), 2)
    shifter = (x_out == got_col[:, None, None] + x_in).astype(jnp.bfloat16)
    shifted = jnp.einsum("kyx,kxX->kyX", got_slabs, shifter, preferred_element_type=jnp.float32)
    shifted = shifted.astype(jnp.bfloat16)
    chips = n_owners // n_halves
    owner_row = jnp.where(got_patch % n_halves == h, chips, 0) + got_patch // n_halves
    owner_of = (
        owner_row[None, :] == jnp.arange(n_owners, dtype=jnp.int32)[:, None]
    ).astype(jnp.bfloat16)
    bands = jnp.dot(
        owner_of, shifted.reshape(entries, band_rows * PS), preferred_element_type=jnp.float32
    ).reshape(n_halves, chips, band_rows, PS)

    per_owner = n_bands * 2
    onehot = (got_patch[:, None] == jnp.arange(n_owners, dtype=jnp.int32)[None, :]).astype(
        jnp.int32
    )
    before = jnp.cumsum(onehot, axis=0) - onehot
    rank = jnp.sum(before * onehot, axis=1)
    target = got_patch * per_owner + rank
    meta_slots = (
        jnp.zeros((n_owners * per_owner, 3), jnp.float32)
        .at[target]
        .set(got_meta[:, 1:], mode="drop")
    )

    pair = bands[1] + lax.ppermute(bands[0], "ec", perm=[(0, 1), (1, 0)])
    recv_bands = lax.all_to_all(pair.astype(jnp.bfloat16), CHIP, split_axis=0, concat_axis=0, tiled=True)
    flux = jnp.sum(recv_bands.astype(jnp.float32), axis=0)
    recv_meta = lax.all_to_all(meta_slots, EXP, split_axis=0, concat_axis=0, tiled=True)

    rows = recv_meta[:, 0].astype(jnp.int32)
    cols = recv_meta[:, 1].astype(jnp.int32)
    wts = recv_meta[:, 2]
    y_index = g * band_rows + jnp.arange(band_rows, dtype=jnp.int32)
    x_index = jnp.arange(PS, dtype=jnp.int32)
    row_mask = (
        (y_index[None, :] >= rows[:, None]) & (y_index[None, :] < rows[:, None] + tile_side)
    ).astype(jnp.float32) * wts[:, None]
    col_mask = (
        (x_index[None, :] >= cols[:, None]) & (x_index[None, :] < cols[:, None] + tile_side)
    ).astype(jnp.float32)
    cover = jnp.einsum("my,mx->yx", row_mask, col_mask, precision=lax.Precision.HIGHEST)
    coadd = flux / jnp.maximum(cover, 1.0)
    return coadd[None]


def solution(mesh):
    n_exp, n_grp = mesh.devices.shape
    n_core = 2
    n_y = 4
    split = Mesh(mesh.devices.reshape(n_y, n_exp // (n_y * n_core), n_core, n_grp), EXP + ("grp",))
    every = EXP + ("grp",)
    in_specs = (
        P(every, None, None),
        P(every),
        P(every, None),
        P(every, None, None),
        P(every, None),
        P(every),
        P(),
        P(),
    )
    out_specs = P(EXP, "grp", None)
    return jax.shard_map(
        per_device, mesh=split, in_specs=in_specs, out_specs=out_specs, check_vma=False
    )
```

```python
import jax
import jax.numpy as jnp
from jax import lax
from jax.sharding import Mesh
from jax.sharding import PartitionSpec as P

PS = 512
EXP = ("ey", "ez", "ec")
CHIP = ("ey", "ez")


def band_matrix(filters, tile_side):
    terms, kernel_width = filters.shape
    half_width = (kernel_width - 1) // 2
    row = lax.broadcasted_iota(jnp.int32, (kernel_width, tile_side, tile_side), 1)
    col = lax.broadcasted_iota(jnp.int32, (kernel_width, tile_side, tile_side), 2)
    tap = lax.broadcasted_iota(jnp.int32, (kernel_width, tile_side, tile_side), 0)
    onehot = (col - row + half_width == tap).astype(jnp.bfloat16)
    band = jnp.einsum("bd,dij->bij", filters, onehot, preferred_element_type=jnp.float32)
    return band.astype(jnp.bfloat16)


def per_device(
    tiles, tile_exposure, tile_patch, tile_offset, coeffs, inv_var, vert_taps, horiz_taps
):
    n_owners = lax.axis_size(EXP)
    n_bands = lax.axis_size("grp")
    tile_count, tile_side, _ = tiles.shape
    listed = tile_patch.shape[1]
    terms = coeffs.shape[1]
    band_rows = PS // n_bands
    g = lax.axis_index("grp")
    h = lax.axis_index("ec")
    n_halves = lax.axis_size("ec")

    packed = jnp.concatenate([coeffs, inv_var[:, None]], axis=1)
    packed = jnp.broadcast_to(packed[None], (n_bands,) + packed.shape)
    packed = lax.all_to_all(packed, "grp", split_axis=0, concat_axis=0, tiled=True)
    packed = packed.reshape(1, -1, terms + 1)
    packed = jnp.broadcast_to(packed, (n_owners,) + packed.shape[1:])
    packed = lax.all_to_all(packed, EXP, split_axis=0, concat_axis=0, tiled=True)
    packed = packed.reshape(-1, terms + 1)

    vband = band_matrix(vert_taps, tile_side)
    hband = band_matrix(horiz_taps, tile_side)

    rows_pass = jnp.einsum("tyk,bxk->tybx", tiles, hband, preferred_element_type=jnp.float32)

    exposures = packed.shape[0]
    picker = (tile_exposure[:, None] == jnp.arange(exposures, dtype=jnp.int32)[None, :]).astype(
        jnp.bfloat16
    )
    picked = jnp.dot(picker, packed, preferred_element_type=jnp.float32)
    coef_tile = picked[:, :terms]
    weight_tile = picked[:, terms]

    partial_value = (rows_pass * coef_tile[:, None, :, None]).astype(jnp.bfloat16)
    smoothed = jnp.einsum(
        "byk,tkbx->tyx", vband, partial_value, preferred_element_type=jnp.float32
    )
    weighted = (weight_tile[:, None, None] * smoothed).astype(jnp.bfloat16)

    row_off = tile_offset[:, :, 0]
    col_off = tile_offset[:, :, 1]
    band_i = lax.broadcasted_iota(jnp.int32, (n_bands, tile_count, listed, band_rows, tile_side), 0)
    inner = lax.broadcasted_iota(jnp.int32, (n_bands, tile_count, listed, band_rows, tile_side), 3)
    src = lax.broadcasted_iota(jnp.int32, (n_bands, tile_count, listed, band_rows, tile_side), 4)
    picks = (src == band_i * band_rows + inner - row_off[None, :, :, None, None]).astype(
        jnp.bfloat16
    )
    slabs = jnp.einsum("gtjiy,tyx->gtjix", picks, weighted, preferred_element_type=jnp.float32)
    slabs = slabs.astype(jnp.bfloat16).reshape(n_bands * tile_count * listed, band_rows, tile_side)
    meta = jnp.stack(
        [
            tile_patch.astype(jnp.float32),
            row_off.astype(jnp.float32),
            col_off.astype(jnp.float32),
            jnp.broadcast_to(weight_tile[:, None], (tile_count, listed)),
        ],
        axis=-1,
    ).reshape(tile_count * listed, 4)
    meta_send = jnp.broadcast_to(meta[None], (n_bands,) + meta.shape).reshape(-1, 4)
    got_slabs = lax.all_to_all(slabs, "grp", split_axis=0, concat_axis=0, tiled=True)
    got_meta = lax.all_to_all(meta_send, "grp", split_axis=0, concat_axis=0, tiled=True)
    entries = got_meta.shape[0]
    got_patch = got_meta[:, 0].astype(jnp.int32)
    got_row = got_meta[:, 1].astype(jnp.int32)
    got_col = got_meta[:, 2].astype(jnp.int32)

    x_in = lax.broadcasted_iota(jnp.int32, (entries, tile_side, PS), 1)
    x_out = lax.broadcasted_iota(jnp.int32, (entries, tile_side, PS), 2)
    shifter = (x_out == got_col[:, None, None] + x_in).astype(jnp.bfloat16)
    shifted = jnp.einsum("kyx,kxX->kyX", got_slabs, shifter, preferred_element_type=jnp.float32)
    shifted = shifted.astype(jnp.bfloat16)
    chips = n_owners // n_halves
    chip_patch = n_halves * jnp.arange(chips, dtype=jnp.int32)[:, None]
    flat_shifted = shifted.reshape(entries, band_rows * PS)
    give_of = (got_patch[None, :] == chip_patch + (1 - h)).astype(jnp.bfloat16)
    give = jnp.dot(give_of, flat_shifted, preferred_element_type=jnp.float32)
    got_give = lax.ppermute(give, "ec", perm=[(0, 1), (1, 0)])
    keep_of = (got_patch[None, :] == chip_patch + h).astype(jnp.bfloat16)
    keep = jnp.dot(keep_of, flat_shifted, preferred_element_type=jnp.float32)

    per_owner = n_bands * 2
    onehot = (got_patch[:, None] == jnp.arange(n_owners, dtype=jnp.int32)[None, :]).astype(
        jnp.int32
    )
    before = jnp.cumsum(onehot, axis=0) - onehot
    rank = jnp.sum(before * onehot, axis=1)
    target = got_patch * per_owner + rank
    meta_slots = (
        jnp.zeros((n_owners * per_owner, 3), jnp.float32)
        .at[target]
        .set(got_meta[:, 1:], mode="drop")
    )

    pair = (keep + got_give).reshape(chips, band_rows, PS)
    recv_bands = lax.all_to_all(pair.astype(jnp.bfloat16), CHIP, split_axis=0, concat_axis=0, tiled=True)
    flux = jnp.sum(recv_bands.astype(jnp.float32), axis=0)
    recv_meta = lax.all_to_all(meta_slots, EXP, split_axis=0, concat_axis=0, tiled=True)

    rows = recv_meta[:, 0].astype(jnp.int32)
    cols = recv_meta[:, 1].astype(jnp.int32)
    wts = recv_meta[:, 2]
    y_index = g * band_rows + jnp.arange(band_rows, dtype=jnp.int32)
    x_index = jnp.arange(PS, dtype=jnp.int32)
    row_mask = (
        (y_index[None, :] >= rows[:, None]) & (y_index[None, :] < rows[:, None] + tile_side)
    ).astype(jnp.float32) * wts[:, None]
    col_mask = (
        (x_index[None, :] >= cols[:, None]) & (x_index[None, :] < cols[:, None] + tile_side)
    ).astype(jnp.float32)
    cover = jnp.einsum("my,mx->yx", row_mask, col_mask, precision=lax.Precision.HIGHEST)
    coadd = flux / jnp.maximum(cover, 1.0)
    return coadd[None]


def solution(mesh):
    n_exp, n_grp = mesh.devices.shape
    n_core = 2
    n_y = 4
    split = Mesh(mesh.devices.reshape(n_y, n_exp // (n_y * n_core), n_core, n_grp), EXP + ("grp",))
    every = EXP + ("grp",)
    in_specs = (
        P(every, None, None),
        P(every),
        P(every, None),
        P(every, None, None),
        P(every, None),
        P(every),
        P(),
        P(),
    )
    out_specs = P(EXP, "grp", None)
    return jax.shard_map(
        per_device, mesh=split, in_specs=in_specs, out_specs=out_specs, check_vma=False
    )
```

```python
import jax
import jax.numpy as jnp
from jax import lax
from jax.sharding import Mesh
from jax.sharding import PartitionSpec as P

PS = 512
EXP = ("ey", "ez", "ec")
CHIP = ("ey", "ez")


def band_matrix(filters, tile_side):
    terms, kernel_width = filters.shape
    half_width = (kernel_width - 1) // 2
    row = lax.broadcasted_iota(jnp.int32, (kernel_width, tile_side, tile_side), 1)
    col = lax.broadcasted_iota(jnp.int32, (kernel_width, tile_side, tile_side), 2)
    tap = lax.broadcasted_iota(jnp.int32, (kernel_width, tile_side, tile_side), 0)
    onehot = (col - row + half_width == tap).astype(jnp.bfloat16)
    band = jnp.einsum("bd,dij->bij", filters, onehot, preferred_element_type=jnp.float32)
    return band.astype(jnp.bfloat16)


def per_device(
    tiles, tile_exposure, tile_patch, tile_offset, coeffs, inv_var, vert_taps, horiz_taps
):
    n_owners = lax.axis_size(EXP)
    n_bands = lax.axis_size("grp")
    tile_count, tile_side, _ = tiles.shape
    listed = tile_patch.shape[1]
    terms = coeffs.shape[1]
    band_rows = PS // n_bands
    g = lax.axis_index("grp")
    h = lax.axis_index("ec")
    n_halves = lax.axis_size("ec")

    packed = jnp.concatenate([coeffs, inv_var[:, None]], axis=1)
    packed = jnp.broadcast_to(packed[None], (n_bands,) + packed.shape)
    packed = lax.all_to_all(packed, "grp", split_axis=0, concat_axis=0, tiled=True)
    packed = packed.reshape(1, -1, terms + 1)
    packed = jnp.broadcast_to(packed, (n_owners,) + packed.shape[1:])
    packed = lax.all_to_all(packed, EXP, split_axis=0, concat_axis=0, tiled=True)
    packed = packed.reshape(-1, terms + 1)

    vband = band_matrix(vert_taps, tile_side)
    hband = band_matrix(horiz_taps, tile_side)

    rows_pass = jnp.einsum("tyk,bxk->tybx", tiles, hband, preferred_element_type=jnp.float32)

    exposures = packed.shape[0]
    picker = (tile_exposure[:, None] == jnp.arange(exposures, dtype=jnp.int32)[None, :]).astype(
        jnp.bfloat16
    )
    picked = jnp.dot(picker, packed, preferred_element_type=jnp.float32)
    coef_tile = picked[:, :terms]
    weight_tile = picked[:, terms]

    partial_value = (rows_pass * coef_tile[:, None, :, None]).astype(jnp.bfloat16)
    smoothed = jnp.einsum(
        "byk,tkbx->tyx", vband, partial_value, preferred_element_type=jnp.float32
    )
    weighted = (weight_tile[:, None, None] * smoothed).astype(jnp.bfloat16)

    row_off = tile_offset[:, :, 0]
    col_off = tile_offset[:, :, 1]
    meta = jnp.stack(
        [
            tile_patch.astype(jnp.float32),
            row_off.astype(jnp.float32),
            col_off.astype(jnp.float32),
            jnp.broadcast_to(weight_tile[:, None], (tile_count, listed)),
        ],
        axis=-1,
    ).reshape(tile_count * listed, 4)
    meta_send = jnp.broadcast_to(meta[None], (n_bands,) + meta.shape).reshape(-1, 4)
    got_meta = lax.all_to_all(meta_send, "grp", split_axis=0, concat_axis=0, tiled=True)
    row_tiles = lax.all_gather(weighted, "grp", axis=0, tiled=True)
    entries = got_meta.shape[0]
    sources = row_tiles.shape[0]
    got_patch = got_meta[:, 0].astype(jnp.int32)
    got_row = got_meta[:, 1].astype(jnp.int32).reshape(sources, listed)
    shape4 = (sources, listed, band_rows, tile_side)
    inner = lax.broadcasted_iota(jnp.int32, shape4, 2)
    src = lax.broadcasted_iota(jnp.int32, shape4, 3)
    picks = (src == g * band_rows + inner - got_row[:, :, None, None]).astype(jnp.bfloat16)
    got_slabs = jnp.einsum("sjiy,syx->sjix", picks, row_tiles, preferred_element_type=jnp.float32)
    got_slabs = got_slabs.astype(jnp.bfloat16).reshape(entries, band_rows, tile_side)
    got_col = got_meta[:, 2].astype(jnp.int32)

    x_in = lax.broadcasted_iota(jnp.int32, (entries, tile_side, PS), 1)
    x_out = lax.broadcasted_iota(jnp.int32, (entries, tile_side, PS), 2)
    shifter = (x_out == got_col[:, None, None] + x_in).astype(jnp.bfloat16)
    shifted = jnp.einsum("kyx,kxX->kyX", got_slabs, shifter, preferred_element_type=jnp.float32)
    shifted = shifted.astype(jnp.bfloat16)
    chips = n_owners // n_halves
    chip_patch = n_halves * jnp.arange(chips, dtype=jnp.int32)[:, None]
    flat_shifted = shifted.reshape(entries, band_rows * PS)
    give_of = (got_patch[None, :] == chip_patch + (1 - h)).astype(jnp.bfloat16)
    give = jnp.dot(give_of, flat_shifted, preferred_element_type=jnp.float32)
    got_give = lax.ppermute(give, "ec", perm=[(0, 1), (1, 0)])
    keep_of = (got_patch[None, :] == chip_patch + h).astype(jnp.bfloat16)
    keep = jnp.dot(keep_of, flat_shifted, preferred_element_type=jnp.float32)

    per_owner = n_bands * 2
    onehot = (got_patch[:, None] == jnp.arange(n_owners, dtype=jnp.int32)[None, :]).astype(
        jnp.int32
    )
    before = jnp.cumsum(onehot, axis=0) - onehot
    rank = jnp.sum(before * onehot, axis=1)
    target = got_patch * per_owner + rank
    meta_slots = (
        jnp.zeros((n_owners * per_owner, 3), jnp.float32)
        .at[target]
        .set(got_meta[:, 1:], mode="drop")
    )

    pair = (keep + got_give).reshape(chips, band_rows, PS)
    recv_bands = lax.all_to_all(pair.astype(jnp.bfloat16), CHIP, split_axis=0, concat_axis=0, tiled=True)
    flux = jnp.sum(recv_bands.astype(jnp.float32), axis=0)
    recv_meta = lax.all_to_all(meta_slots, EXP, split_axis=0, concat_axis=0, tiled=True)

    rows = recv_meta[:, 0].astype(jnp.int32)
    cols = recv_meta[:, 1].astype(jnp.int32)
    wts = recv_meta[:, 2]
    y_index = g * band_rows + jnp.arange(band_rows, dtype=jnp.int32)
    x_index = jnp.arange(PS, dtype=jnp.int32)
    row_mask = (
        (y_index[None, :] >= rows[:, None]) & (y_index[None, :] < rows[:, None] + tile_side)
    ).astype(jnp.float32) * wts[:, None]
    col_mask = (
        (x_index[None, :] >= cols[:, None]) & (x_index[None, :] < cols[:, None] + tile_side)
    ).astype(jnp.float32)
    cover = jnp.einsum("my,mx->yx", row_mask, col_mask, precision=lax.Precision.HIGHEST)
    coadd = flux / jnp.maximum(cover, 1.0)
    return coadd[None]


def solution(mesh):
    n_exp, n_grp = mesh.devices.shape
    n_core = 2
    n_y = 4
    split = Mesh(mesh.devices.reshape(n_y, n_exp // (n_y * n_core), n_core, n_grp), EXP + ("grp",))
    every = EXP + ("grp",)
    in_specs = (
        P(every, None, None),
        P(every),
        P(every, None),
        P(every, None, None),
        P(every, None),
        P(every),
        P(),
        P(),
    )
    out_specs = P(EXP, "grp", None)
    return jax.shard_map(
        per_device, mesh=split, in_specs=in_specs, out_specs=out_specs, check_vma=False
    )
```

```python
import jax
import jax.numpy as jnp
from jax import lax
from jax.sharding import Mesh
from jax.sharding import PartitionSpec as P

PS = 512
EXP = ("ey", "ez", "ec")
CHIP = ("ey", "ez")


def band_matrix(filters, tile_side):
    terms, kernel_width = filters.shape
    half_width = (kernel_width - 1) // 2
    row = lax.broadcasted_iota(jnp.int32, (kernel_width, tile_side, tile_side), 1)
    col = lax.broadcasted_iota(jnp.int32, (kernel_width, tile_side, tile_side), 2)
    tap = lax.broadcasted_iota(jnp.int32, (kernel_width, tile_side, tile_side), 0)
    onehot = (col - row + half_width == tap).astype(jnp.bfloat16)
    band = jnp.einsum("bd,dij->bij", filters, onehot, preferred_element_type=jnp.float32)
    return band.astype(jnp.bfloat16)


def per_device(
    tiles, tile_exposure, tile_patch, tile_offset, coeffs, inv_var, vert_taps, horiz_taps
):
    n_owners = lax.axis_size(EXP)
    n_bands = lax.axis_size("grp")
    tile_count, tile_side, _ = tiles.shape
    listed = tile_patch.shape[1]
    terms = coeffs.shape[1]
    band_rows = PS // n_bands
    g = lax.axis_index("grp")
    h = lax.axis_index("ec")
    n_halves = lax.axis_size("ec")

    n_dev = n_owners * n_bands
    packed = jnp.concatenate([coeffs, inv_var[:, None]], axis=1).astype(jnp.float32)
    own_entries = jnp.stack(
        [
            tile_patch,
            tile_offset[:, :, 0],
            tile_offset[:, :, 1],
            jnp.broadcast_to(tile_exposure[:, None], (tile_count, listed)),
        ],
        axis=-1,
    ).astype(jnp.float32)
    payload = jnp.concatenate([packed.reshape(-1), own_entries.reshape(-1)])
    width = payload.shape[0]
    payload = jnp.broadcast_to(payload[None], (n_bands, width))
    payload = lax.all_to_all(payload, "grp", split_axis=0, concat_axis=0, tiled=True)
    payload = jnp.broadcast_to(payload.reshape(1, 1, n_bands * width), (n_owners, 1, n_bands * width))
    payload = lax.all_to_all(payload, EXP, split_axis=0, concat_axis=0, tiled=True)
    payload = payload.reshape(n_dev, width)
    per_dev_coef = packed.size
    packed = payload[:, :per_dev_coef].reshape(-1, terms + 1).astype(jnp.bfloat16)
    all_entries = payload[:, per_dev_coef:].reshape(n_dev * tile_count * listed, 4)

    vband = band_matrix(vert_taps, tile_side)
    hband = band_matrix(horiz_taps, tile_side)

    rows_pass = jnp.einsum("tyk,bxk->tybx", tiles, hband, preferred_element_type=jnp.float32)

    exposures = packed.shape[0]
    picker = (tile_exposure[:, None] == jnp.arange(exposures, dtype=jnp.int32)[None, :]).astype(
        jnp.bfloat16
    )
    picked = jnp.dot(picker, packed, preferred_element_type=jnp.float32)
    coef_tile = picked[:, :terms]
    weight_tile = picked[:, terms]

    partial_value = (rows_pass * coef_tile[:, None, :, None]).astype(jnp.bfloat16)
    smoothed = jnp.einsum(
        "byk,tkbx->tyx", vband, partial_value, preferred_element_type=jnp.float32
    )
    weighted = (weight_tile[:, None, None] * smoothed).astype(jnp.bfloat16)

    e = lax.axis_index(EXP)
    row_entries = n_bands * tile_count * listed
    got_meta = lax.dynamic_slice_in_dim(all_entries, e * row_entries, row_entries, axis=0)
    row_tiles = lax.all_gather(weighted, "grp", axis=0, tiled=True)
    entries = got_meta.shape[0]
    sources = row_tiles.shape[0]
    got_patch = got_meta[:, 0].astype(jnp.int32)
    got_row = got_meta[:, 1].astype(jnp.int32).reshape(sources, listed)
    shape4 = (sources, listed, band_rows, tile_side)
    inner = lax.broadcasted_iota(jnp.int32, shape4, 2)
    src = lax.broadcasted_iota(jnp.int32, shape4, 3)
    picks = (src == g * band_rows + inner - got_row[:, :, None, None]).astype(jnp.bfloat16)
    got_slabs = jnp.einsum("sjiy,syx->sjix", picks, row_tiles, preferred_element_type=jnp.float32)
    got_slabs = got_slabs.astype(jnp.bfloat16).reshape(entries, band_rows, tile_side)
    got_col = got_meta[:, 2].astype(jnp.int32)

    x_in = lax.broadcasted_iota(jnp.int32, (entries, tile_side, PS), 1)
    x_out = lax.broadcasted_iota(jnp.int32, (entries, tile_side, PS), 2)
    shifter = (x_out == got_col[:, None, None] + x_in).astype(jnp.bfloat16)
    shifted = jnp.einsum("kyx,kxX->kyX", got_slabs, shifter, preferred_element_type=jnp.float32)
    shifted = shifted.astype(jnp.bfloat16)
    chips = n_owners // n_halves
    chip_patch = n_halves * jnp.arange(chips, dtype=jnp.int32)[:, None]
    flat_shifted = shifted.reshape(entries, band_rows * PS)
    give_of = (got_patch[None, :] == chip_patch + (1 - h)).astype(jnp.bfloat16)
    give = jnp.dot(give_of, flat_shifted, preferred_element_type=jnp.float32)
    got_give = lax.ppermute(give, "ec", perm=[(0, 1), (1, 0)])
    keep_of = (got_patch[None, :] == chip_patch + h).astype(jnp.bfloat16)
    keep = jnp.dot(keep_of, flat_shifted, preferred_element_type=jnp.float32)

    pair = (keep + got_give).reshape(chips, band_rows, PS)
    recv_bands = lax.all_to_all(pair.astype(jnp.bfloat16), CHIP, split_axis=0, concat_axis=0, tiled=True)
    flux = jnp.sum(recv_bands.astype(jnp.float32), axis=0)
    rows = all_entries[:, 1].astype(jnp.int32)
    cols = all_entries[:, 2].astype(jnp.int32)
    entry_exposure = all_entries[:, 3].astype(jnp.int32)
    exposure_pick = (
        entry_exposure[:, None] == jnp.arange(exposures, dtype=jnp.int32)[None, :]
    ).astype(jnp.bfloat16)
    wts = jnp.dot(exposure_pick, packed[:, terms], preferred_element_type=jnp.float32)
    wts = jnp.where(all_entries[:, 0].astype(jnp.int32) == e, wts, 0.0)
    y_index = g * band_rows + jnp.arange(band_rows, dtype=jnp.int32)
    x_index = jnp.arange(PS, dtype=jnp.int32)
    row_mask = (
        (y_index[None, :] >= rows[:, None]) & (y_index[None, :] < rows[:, None] + tile_side)
    ).astype(jnp.float32) * wts[:, None]
    col_mask = (
        (x_index[None, :] >= cols[:, None]) & (x_index[None, :] < cols[:, None] + tile_side)
    ).astype(jnp.float32)
    cover = jnp.einsum(
        "my,mx->yx",
        row_mask.astype(jnp.bfloat16),
        col_mask.astype(jnp.bfloat16),
        preferred_element_type=jnp.float32,
    )
    coadd = flux / jnp.maximum(cover, 1.0)
    return coadd[None]


def solution(mesh):
    n_exp, n_grp = mesh.devices.shape
    n_core = 2
    n_y = 4
    split = Mesh(mesh.devices.reshape(n_y, n_exp // (n_y * n_core), n_core, n_grp), EXP + ("grp",))
    every = EXP + ("grp",)
    in_specs = (
        P(every, None, None),
        P(every),
        P(every, None),
        P(every, None, None),
        P(every, None),
        P(every),
        P(),
        P(),
    )
    out_specs = P(EXP, "grp", None)
    return jax.shard_map(
        per_device, mesh=split, in_specs=in_specs, out_specs=out_specs, check_vma=False
    )
```

```python
import jax
import jax.numpy as jnp
from jax import lax
from jax.sharding import Mesh
from jax.sharding import PartitionSpec as P

PS = 512
EXP = ("ey", "ez", "ec")
CHIP = ("ey", "ez")


def band_matrix(filters, tile_side):
    terms, kernel_width = filters.shape
    half_width = (kernel_width - 1) // 2
    row = lax.broadcasted_iota(jnp.int32, (kernel_width, tile_side, tile_side), 1)
    col = lax.broadcasted_iota(jnp.int32, (kernel_width, tile_side, tile_side), 2)
    tap = lax.broadcasted_iota(jnp.int32, (kernel_width, tile_side, tile_side), 0)
    onehot = (col - row + half_width == tap).astype(jnp.bfloat16)
    band = jnp.einsum("bd,dij->bij", filters, onehot, preferred_element_type=jnp.float32)
    return band.astype(jnp.bfloat16)


def per_device(
    tiles, tile_exposure, tile_patch, tile_offset, coeffs, inv_var, vert_taps, horiz_taps
):
    n_owners = lax.axis_size(EXP)
    n_bands = lax.axis_size("grp")
    tile_count, tile_side, _ = tiles.shape
    listed = tile_patch.shape[1]
    terms = coeffs.shape[1]
    band_rows = PS // n_bands
    g = lax.axis_index("grp")
    h = lax.axis_index("ec")
    n_halves = lax.axis_size("ec")

    n_dev = n_owners * n_bands
    packed = jnp.concatenate([coeffs, inv_var[:, None]], axis=1).astype(jnp.float32)
    own_entries = jnp.stack(
        [
            tile_patch,
            tile_offset[:, :, 0],
            tile_offset[:, :, 1],
            jnp.broadcast_to(tile_exposure[:, None], (tile_count, listed)),
        ],
        axis=-1,
    ).astype(jnp.float32)
    payload = jnp.concatenate([packed.reshape(-1), own_entries.reshape(-1)])
    width = payload.shape[0]
    payload = jnp.broadcast_to(payload[None], (n_bands, width))
    payload = lax.all_to_all(payload, "grp", split_axis=0, concat_axis=0, tiled=True)
    payload = jnp.broadcast_to(payload.reshape(1, 1, n_bands * width), (n_owners, 1, n_bands * width))
    payload = lax.all_to_all(payload, EXP, split_axis=0, concat_axis=0, tiled=True)
    payload = payload.reshape(n_dev, width)
    per_dev_coef = packed.size
    packed = payload[:, :per_dev_coef].reshape(-1, terms + 1).astype(jnp.bfloat16)
    all_entries = payload[:, per_dev_coef:].reshape(n_dev * tile_count * listed, 4)

    vband = band_matrix(vert_taps, tile_side)
    hband = band_matrix(horiz_taps, tile_side)

    rows_pass = jnp.einsum("tyk,bxk->tybx", tiles, hband, preferred_element_type=jnp.float32)

    exposures = packed.shape[0]
    picker = (tile_exposure[:, None] == jnp.arange(exposures, dtype=jnp.int32)[None, :]).astype(
        jnp.bfloat16
    )
    picked = jnp.dot(picker, packed, preferred_element_type=jnp.float32)
    coef_tile = picked[:, :terms]
    weight_tile = picked[:, terms]

    partial_value = (rows_pass * coef_tile[:, None, :, None]).astype(jnp.bfloat16)
    smoothed = jnp.einsum(
        "byk,tkbx->tyx", vband, partial_value, preferred_element_type=jnp.float32
    )
    weighted = (weight_tile[:, None, None] * smoothed).astype(jnp.bfloat16)

    e = lax.axis_index(EXP)
    row_entries = n_bands * tile_count * listed
    got_meta = lax.dynamic_slice_in_dim(all_entries, e * row_entries, row_entries, axis=0)
    row_tiles = lax.all_gather(weighted, "grp", axis=0, tiled=True)
    entries = got_meta.shape[0]
    sources = row_tiles.shape[0]
    got_patch = got_meta[:, 0].astype(jnp.int32)
    got_row = got_meta[:, 1].astype(jnp.int32).reshape(sources, listed)
    shape4 = (sources, listed, band_rows, tile_side)
    inner = lax.broadcasted_iota(jnp.int32, shape4, 2)
    src = lax.broadcasted_iota(jnp.int32, shape4, 3)
    picks = (src == g * band_rows + inner - got_row[:, :, None, None]).astype(jnp.bfloat16)
    got_slabs = jnp.einsum("sjiy,syx->sjix", picks, row_tiles, preferred_element_type=jnp.float32)
    got_slabs = got_slabs.astype(jnp.bfloat16).reshape(entries, band_rows, tile_side)
    got_col = got_meta[:, 2].astype(jnp.int32)

    x_in = lax.broadcasted_iota(jnp.int32, (entries, tile_side, PS), 1)
    x_out = lax.broadcasted_iota(jnp.int32, (entries, tile_side, PS), 2)
    shifter = (x_out == got_col[:, None, None] + x_in).astype(jnp.bfloat16)
    shifted = jnp.einsum("kyx,kxX->kyX", got_slabs, shifter, preferred_element_type=jnp.float32)
    shifted = shifted.astype(jnp.bfloat16)
    chips = n_owners // n_halves
    chip_patch = n_halves * jnp.arange(chips, dtype=jnp.int32)[:, None]
    flat_shifted = shifted.reshape(entries, band_rows * PS)
    give_of = (got_patch[None, :] == chip_patch + (1 - h)).astype(jnp.bfloat16)
    give = jnp.dot(give_of, flat_shifted, preferred_element_type=jnp.float32)
    got_give = lax.ppermute(give.astype(jnp.bfloat16), "ec", perm=[(0, 1), (1, 0)])
    keep_of = (got_patch[None, :] == chip_patch + h).astype(jnp.bfloat16)
    keep = jnp.dot(keep_of, flat_shifted, preferred_element_type=jnp.float32)

    pair = (keep + got_give.astype(jnp.float32)).reshape(chips, band_rows, PS)
    recv_bands = lax.all_to_all(pair.astype(jnp.bfloat16), CHIP, split_axis=0, concat_axis=0, tiled=True)
    flux = jnp.sum(recv_bands.astype(jnp.float32), axis=0)
    rows = all_entries[:, 1].astype(jnp.int32)
    cols = all_entries[:, 2].astype(jnp.int32)
    entry_exposure = all_entries[:, 3].astype(jnp.int32)
    exposure_pick = (
        entry_exposure[:, None] == jnp.arange(exposures, dtype=jnp.int32)[None, :]
    ).astype(jnp.bfloat16)
    wts = jnp.dot(exposure_pick, packed[:, terms], preferred_element_type=jnp.float32)
    wts = jnp.where(all_entries[:, 0].astype(jnp.int32) == e, wts, 0.0)
    y_index = g * band_rows + jnp.arange(band_rows, dtype=jnp.int32)
    x_index = jnp.arange(PS, dtype=jnp.int32)
    row_mask = (
        (y_index[None, :] >= rows[:, None]) & (y_index[None, :] < rows[:, None] + tile_side)
    ).astype(jnp.float32) * wts[:, None]
    col_mask = (
        (x_index[None, :] >= cols[:, None]) & (x_index[None, :] < cols[:, None] + tile_side)
    ).astype(jnp.float32)
    cover = jnp.einsum(
        "my,mx->yx",
        row_mask.astype(jnp.bfloat16),
        col_mask.astype(jnp.bfloat16),
        preferred_element_type=jnp.float32,
    )
    cover = lax.optimization_barrier(cover)
    coadd = flux / jnp.maximum(cover, 1.0)
    return coadd[None]


def solution(mesh):
    n_exp, n_grp = mesh.devices.shape
    n_core = 2
    n_y = 4
    split = Mesh(mesh.devices.reshape(n_y, n_exp // (n_y * n_core), n_core, n_grp), EXP + ("grp",))
    every = EXP + ("grp",)
    in_specs = (
        P(every, None, None),
        P(every),
        P(every, None),
        P(every, None, None),
        P(every, None),
        P(every),
        P(),
        P(),
    )
    out_specs = P(EXP, "grp", None)
    return jax.shard_map(
        per_device, mesh=split, in_specs=in_specs, out_specs=out_specs, check_vma=False
    )
```

```python
import jax
import jax.numpy as jnp
from jax import lax
from jax.sharding import Mesh
from jax.sharding import PartitionSpec as P

PS = 512
EXP = ("ey", "ez", "ec")
CHIP = ("ey", "ez")


def band_matrix(filters, tile_side):
    terms, kernel_width = filters.shape
    half_width = (kernel_width - 1) // 2
    row = lax.broadcasted_iota(jnp.int32, (kernel_width, tile_side, tile_side), 1)
    col = lax.broadcasted_iota(jnp.int32, (kernel_width, tile_side, tile_side), 2)
    tap = lax.broadcasted_iota(jnp.int32, (kernel_width, tile_side, tile_side), 0)
    onehot = (col - row + half_width == tap).astype(jnp.bfloat16)
    band = jnp.einsum("bd,dij->bij", filters, onehot, preferred_element_type=jnp.float32)
    return band.astype(jnp.bfloat16)


def per_device(
    tiles, tile_exposure, tile_patch, tile_offset, coeffs, inv_var, vert_taps, horiz_taps
):
    n_owners = lax.axis_size(EXP)
    n_bands = lax.axis_size("grp")
    tile_count, tile_side, _ = tiles.shape
    listed = tile_patch.shape[1]
    terms = coeffs.shape[1]
    band_rows = PS // n_bands
    g = lax.axis_index("grp")
    h = lax.axis_index("ec")
    n_halves = lax.axis_size("ec")

    n_dev = n_owners * n_bands
    packed = jnp.concatenate([coeffs, inv_var[:, None]], axis=1).astype(jnp.float32)
    own_entries = jnp.stack(
        [
            tile_patch,
            tile_offset[:, :, 0],
            tile_offset[:, :, 1],
            jnp.broadcast_to(tile_exposure[:, None], (tile_count, listed)),
        ],
        axis=-1,
    ).astype(jnp.float32)
    payload = jnp.concatenate([packed.reshape(-1), own_entries.reshape(-1)])
    width = payload.shape[0]
    payload = jnp.broadcast_to(payload[None], (n_bands, width))
    payload = lax.all_to_all(payload, "grp", split_axis=0, concat_axis=0, tiled=True)
    payload = jnp.broadcast_to(payload.reshape(1, 1, n_bands * width), (n_owners, 1, n_bands * width))
    payload = lax.all_to_all(payload, EXP, split_axis=0, concat_axis=0, tiled=True)
    payload = payload.reshape(n_dev, width)
    per_dev_coef = packed.size
    packed = payload[:, :per_dev_coef].reshape(-1, terms + 1).astype(jnp.bfloat16)
    all_entries = payload[:, per_dev_coef:].reshape(n_dev * tile_count * listed, 4)

    vband = band_matrix(vert_taps, tile_side)
    hband = band_matrix(horiz_taps, tile_side)

    e = lax.axis_index(EXP)
    row_entries = n_bands * tile_count * listed
    got_meta = lax.dynamic_slice_in_dim(all_entries, e * row_entries, row_entries, axis=0)
    row_raw = lax.all_gather(tiles, "grp", axis=0, tiled=True)
    sources = row_raw.shape[0]
    row_exposure = got_meta[:, 3].astype(jnp.int32).reshape(sources, listed)[:, 0]

    rows_pass = jnp.einsum("tyk,bxk->tybx", row_raw, hband, preferred_element_type=jnp.float32)

    exposures = packed.shape[0]
    picker = (row_exposure[:, None] == jnp.arange(exposures, dtype=jnp.int32)[None, :]).astype(
        jnp.bfloat16
    )
    picked = jnp.dot(picker, packed, preferred_element_type=jnp.float32)
    coef_tile = picked[:, :terms]
    weight_tile = picked[:, terms]

    partial_value = (rows_pass * coef_tile[:, None, :, None]).astype(jnp.bfloat16)
    smoothed = jnp.einsum(
        "byk,tkbx->tyx", vband, partial_value, preferred_element_type=jnp.float32
    )
    row_tiles = (weight_tile[:, None, None] * smoothed).astype(jnp.bfloat16)

    entries = got_meta.shape[0]
    got_patch = got_meta[:, 0].astype(jnp.int32)
    got_row = got_meta[:, 1].astype(jnp.int32).reshape(sources, listed)
    shape4 = (sources, listed, band_rows, tile_side)
    inner = lax.broadcasted_iota(jnp.int32, shape4, 2)
    src = lax.broadcasted_iota(jnp.int32, shape4, 3)
    picks = (src == g * band_rows + inner - got_row[:, :, None, None]).astype(jnp.bfloat16)
    got_slabs = jnp.einsum("sjiy,syx->sjix", picks, row_tiles, preferred_element_type=jnp.float32)
    got_slabs = got_slabs.astype(jnp.bfloat16).reshape(entries, band_rows, tile_side)
    got_col = got_meta[:, 2].astype(jnp.int32)

    x_in = lax.broadcasted_iota(jnp.int32, (entries, tile_side, PS), 1)
    x_out = lax.broadcasted_iota(jnp.int32, (entries, tile_side, PS), 2)
    shifter = (x_out == got_col[:, None, None] + x_in).astype(jnp.bfloat16)
    shifted = jnp.einsum("kyx,kxX->kyX", got_slabs, shifter, preferred_element_type=jnp.float32)
    shifted = shifted.astype(jnp.bfloat16)
    chips = n_owners // n_halves
    chip_patch = n_halves * jnp.arange(chips, dtype=jnp.int32)[:, None]
    flat_shifted = shifted.reshape(entries, band_rows * PS)
    give_of = (got_patch[None, :] == chip_patch + (1 - h)).astype(jnp.bfloat16)
    give = jnp.dot(give_of, flat_shifted, preferred_element_type=jnp.float32)
    got_give = lax.ppermute(give.astype(jnp.bfloat16), "ec", perm=[(0, 1), (1, 0)])
    keep_of = (got_patch[None, :] == chip_patch + h).astype(jnp.bfloat16)
    keep = jnp.dot(keep_of, flat_shifted, preferred_element_type=jnp.float32)

    pair = (keep + got_give.astype(jnp.float32)).reshape(chips, band_rows, PS)
    recv_bands = lax.all_to_all(pair.astype(jnp.bfloat16), CHIP, split_axis=0, concat_axis=0, tiled=True)
    flux = jnp.sum(recv_bands.astype(jnp.float32), axis=0)
    rows = all_entries[:, 1].astype(jnp.int32)
    cols = all_entries[:, 2].astype(jnp.int32)
    entry_exposure = all_entries[:, 3].astype(jnp.int32)
    exposure_pick = (
        entry_exposure[:, None] == jnp.arange(exposures, dtype=jnp.int32)[None, :]
    ).astype(jnp.bfloat16)
    wts = jnp.dot(exposure_pick, packed[:, terms], preferred_element_type=jnp.float32)
    wts = jnp.where(all_entries[:, 0].astype(jnp.int32) == e, wts, 0.0)
    y_index = g * band_rows + jnp.arange(band_rows, dtype=jnp.int32)
    x_index = jnp.arange(PS, dtype=jnp.int32)
    row_mask = (
        (y_index[None, :] >= rows[:, None]) & (y_index[None, :] < rows[:, None] + tile_side)
    ).astype(jnp.float32) * wts[:, None]
    col_mask = (
        (x_index[None, :] >= cols[:, None]) & (x_index[None, :] < cols[:, None] + tile_side)
    ).astype(jnp.float32)
    cover = jnp.einsum(
        "my,mx->yx",
        row_mask.astype(jnp.bfloat16),
        col_mask.astype(jnp.bfloat16),
        preferred_element_type=jnp.float32,
    )
    cover = lax.optimization_barrier(cover)
    coadd = flux / jnp.maximum(cover, 1.0)
    return coadd[None]


def solution(mesh):
    n_exp, n_grp = mesh.devices.shape
    n_core = 2
    n_y = 4
    split = Mesh(mesh.devices.reshape(n_y, n_exp // (n_y * n_core), n_core, n_grp), EXP + ("grp",))
    every = EXP + ("grp",)
    in_specs = (
        P(every, None, None),
        P(every),
        P(every, None),
        P(every, None, None),
        P(every, None),
        P(every),
        P(),
        P(),
    )
    out_specs = P(EXP, "grp", None)
    return jax.shard_map(
        per_device, mesh=split, in_specs=in_specs, out_specs=out_specs, check_vma=False
    )
```

```python
import jax
import jax.numpy as jnp
from jax import lax
from jax.sharding import Mesh
from jax.sharding import PartitionSpec as P

PS = 512
EXP = ("ey", "ez", "ec")
CHIP = ("ey", "ez")


def band_matrix(filters, tile_side):
    terms, kernel_width = filters.shape
    half_width = (kernel_width - 1) // 2
    row = lax.broadcasted_iota(jnp.int32, (kernel_width, tile_side, tile_side), 1)
    col = lax.broadcasted_iota(jnp.int32, (kernel_width, tile_side, tile_side), 2)
    tap = lax.broadcasted_iota(jnp.int32, (kernel_width, tile_side, tile_side), 0)
    onehot = (col - row + half_width == tap).astype(jnp.bfloat16)
    band = jnp.einsum("bd,dij->bij", filters, onehot, preferred_element_type=jnp.float32)
    return band.astype(jnp.bfloat16)


def per_device(
    tiles, tile_exposure, tile_patch, tile_offset, coeffs, inv_var, vert_taps, horiz_taps
):
    n_owners = lax.axis_size(EXP)
    n_bands = lax.axis_size("grp")
    tile_count, tile_side, _ = tiles.shape
    listed = tile_patch.shape[1]
    terms = coeffs.shape[1]
    band_rows = PS // n_bands
    g = lax.axis_index("grp")
    h = lax.axis_index("ec")
    n_halves = lax.axis_size("ec")

    n_dev = n_owners * n_bands
    packed = jnp.concatenate([coeffs, inv_var[:, None]], axis=1).astype(jnp.float32)
    own_entries = jnp.stack(
        [
            tile_patch,
            tile_offset[:, :, 0],
            tile_offset[:, :, 1],
            jnp.broadcast_to(tile_exposure[:, None], (tile_count, listed)),
        ],
        axis=-1,
    ).astype(jnp.float32)
    payload = jnp.concatenate([packed.reshape(-1), own_entries.reshape(-1)])
    width = payload.shape[0]
    payload = jnp.broadcast_to(payload[None], (n_bands, width))
    payload = lax.all_to_all(payload, "grp", split_axis=0, concat_axis=0, tiled=True)
    payload = jnp.broadcast_to(payload.reshape(1, 1, n_bands * width), (n_owners, 1, n_bands * width))
    payload = lax.all_to_all(payload, EXP, split_axis=0, concat_axis=0, tiled=True)
    payload = payload.reshape(n_dev, width)
    per_dev_coef = packed.size
    packed = payload[:, :per_dev_coef].reshape(-1, terms + 1).astype(jnp.bfloat16)
    all_entries = payload[:, per_dev_coef:].reshape(n_dev * tile_count * listed, 4)

    vband = band_matrix(vert_taps, tile_side)
    hband = band_matrix(horiz_taps, tile_side)

    rows_pass = jnp.einsum("tyk,bxk->tybx", tiles, hband, preferred_element_type=jnp.float32)
    rows_pass = lax.optimization_barrier(rows_pass)

    exposures = packed.shape[0]
    picker = (tile_exposure[:, None] == jnp.arange(exposures, dtype=jnp.int32)[None, :]).astype(
        jnp.bfloat16
    )
    picked = jnp.dot(picker, packed, preferred_element_type=jnp.float32)
    coef_tile = picked[:, :terms]
    weight_tile = picked[:, terms]

    partial_value = (rows_pass * coef_tile[:, None, :, None]).astype(jnp.bfloat16)
    smoothed = jnp.einsum(
        "byk,tkbx->tyx", vband, partial_value, preferred_element_type=jnp.float32
    )
    weighted = (weight_tile[:, None, None] * smoothed).astype(jnp.bfloat16)

    e = lax.axis_index(EXP)
    row_entries = n_bands * tile_count * listed
    got_meta = lax.dynamic_slice_in_dim(all_entries, e * row_entries, row_entries, axis=0)
    row_tiles = lax.all_gather(weighted, "grp", axis=0, tiled=True)
    entries = got_meta.shape[0]
    sources = row_tiles.shape[0]
    got_patch = got_meta[:, 0].astype(jnp.int32)
    got_row = got_meta[:, 1].astype(jnp.int32).reshape(sources, listed)
    shape4 = (sources, listed, band_rows, tile_side)
    inner = lax.broadcasted_iota(jnp.int32, shape4, 2)
    src = lax.broadcasted_iota(jnp.int32, shape4, 3)
    picks = (src == g * band_rows + inner - got_row[:, :, None, None]).astype(jnp.bfloat16)
    got_slabs = jnp.einsum("sjiy,syx->sjix", picks, row_tiles, preferred_element_type=jnp.float32)
    got_slabs = got_slabs.astype(jnp.bfloat16).reshape(entries, band_rows, tile_side)
    got_col = got_meta[:, 2].astype(jnp.int32)

    x_in = lax.broadcasted_iota(jnp.int32, (entries, tile_side, PS), 1)
    x_out = lax.broadcasted_iota(jnp.int32, (entries, tile_side, PS), 2)
    shifter = (x_out == got_col[:, None, None] + x_in).astype(jnp.bfloat16)
    shifted = jnp.einsum("kyx,kxX->kyX", got_slabs, shifter, preferred_element_type=jnp.float32)
    shifted = shifted.astype(jnp.bfloat16)
    chips = n_owners // n_halves
    chip_patch = n_halves * jnp.arange(chips, dtype=jnp.int32)[:, None]
    flat_shifted = shifted.reshape(entries, band_rows * PS)
    give_of = (got_patch[None, :] == chip_patch + (1 - h)).astype(jnp.bfloat16)
    give = jnp.dot(give_of, flat_shifted, preferred_element_type=jnp.float32)
    got_give = lax.ppermute(give.astype(jnp.bfloat16), "ec", perm=[(0, 1), (1, 0)])
    keep_of = (got_patch[None, :] == chip_patch + h).astype(jnp.bfloat16)
    keep = jnp.dot(keep_of, flat_shifted, preferred_element_type=jnp.float32)

    pair = (keep + got_give.astype(jnp.float32)).reshape(chips, band_rows, PS)
    recv_bands = lax.all_to_all(pair.astype(jnp.bfloat16), CHIP, split_axis=0, concat_axis=0, tiled=True)
    flux = jnp.sum(recv_bands.astype(jnp.float32), axis=0)
    rows = all_entries[:, 1].astype(jnp.int32)
    cols = all_entries[:, 2].astype(jnp.int32)
    entry_exposure = all_entries[:, 3].astype(jnp.int32)
    exposure_pick = (
        entry_exposure[:, None] == jnp.arange(exposures, dtype=jnp.int32)[None, :]
    ).astype(jnp.bfloat16)
    wts = jnp.dot(exposure_pick, packed[:, terms], preferred_element_type=jnp.float32)
    wts = jnp.where(all_entries[:, 0].astype(jnp.int32) == e, wts, 0.0)
    y_index = g * band_rows + jnp.arange(band_rows, dtype=jnp.int32)
    x_index = jnp.arange(PS, dtype=jnp.int32)
    row_mask = (
        (y_index[None, :] >= rows[:, None]) & (y_index[None, :] < rows[:, None] + tile_side)
    ).astype(jnp.float32) * wts[:, None]
    col_mask = (
        (x_index[None, :] >= cols[:, None]) & (x_index[None, :] < cols[:, None] + tile_side)
    ).astype(jnp.float32)
    cover = jnp.einsum(
        "my,mx->yx",
        row_mask.astype(jnp.bfloat16),
        col_mask.astype(jnp.bfloat16),
        preferred_element_type=jnp.float32,
    )
    cover = lax.optimization_barrier(cover)
    coadd = flux / jnp.maximum(cover, 1.0)
    return coadd[None]


def solution(mesh):
    n_exp, n_grp = mesh.devices.shape
    n_core = 2
    n_y = 4
    split = Mesh(mesh.devices.reshape(n_y, n_exp // (n_y * n_core), n_core, n_grp), EXP + ("grp",))
    every = EXP + ("grp",)
    in_specs = (
        P(every, None, None),
        P(every),
        P(every, None),
        P(every, None, None),
        P(every, None),
        P(every),
        P(),
        P(),
    )
    out_specs = P(EXP, "grp", None)
    return jax.shard_map(
        per_device, mesh=split, in_specs=in_specs, out_specs=out_specs, check_vma=False
    )
```

```python
import jax
import jax.numpy as jnp
from jax import lax
from jax.sharding import Mesh
from jax.sharding import PartitionSpec as P

PS = 512
EXP = ("ey", "ez", "ec")
CHIP = ("ey", "ez")


def band_matrix(filters, tile_side):
    terms, kernel_width = filters.shape
    half_width = (kernel_width - 1) // 2
    row = lax.broadcasted_iota(jnp.int32, (kernel_width, tile_side, tile_side), 1)
    col = lax.broadcasted_iota(jnp.int32, (kernel_width, tile_side, tile_side), 2)
    tap = lax.broadcasted_iota(jnp.int32, (kernel_width, tile_side, tile_side), 0)
    onehot = (col - row + half_width == tap).astype(jnp.bfloat16)
    band = jnp.einsum("bd,dij->bij", filters, onehot, preferred_element_type=jnp.float32)
    return band.astype(jnp.bfloat16)


def per_device(
    tiles, tile_exposure, tile_patch, tile_offset, coeffs, inv_var, vert_taps, horiz_taps
):
    n_owners = lax.axis_size(EXP)
    n_bands = lax.axis_size("grp")
    tile_count, tile_side, _ = tiles.shape
    listed = tile_patch.shape[1]
    terms = coeffs.shape[1]
    band_rows = PS // n_bands
    g = lax.axis_index("grp")
    h = lax.axis_index("ec")
    n_halves = lax.axis_size("ec")

    n_dev = n_owners * n_bands
    packed = jnp.concatenate([coeffs, inv_var[:, None]], axis=1).astype(jnp.float32)
    own_entries = jnp.stack(
        [
            tile_patch,
            tile_offset[:, :, 0],
            tile_offset[:, :, 1],
            jnp.broadcast_to(tile_exposure[:, None], (tile_count, listed)),
        ],
        axis=-1,
    ).astype(jnp.float32)
    payload = jnp.concatenate([packed.reshape(-1), own_entries.reshape(-1)])
    width = payload.shape[0]
    payload = jnp.broadcast_to(payload[None], (n_bands, width))
    payload = lax.all_to_all(payload, "grp", split_axis=0, concat_axis=0, tiled=True)
    payload = jnp.broadcast_to(payload.reshape(1, 1, n_bands * width), (n_owners, 1, n_bands * width))
    payload = lax.all_to_all(payload, EXP, split_axis=0, concat_axis=0, tiled=True)
    payload = payload.reshape(n_dev, width)
    per_dev_coef = packed.size
    packed = payload[:, :per_dev_coef].reshape(-1, terms + 1).astype(jnp.bfloat16)
    all_entries = payload[:, per_dev_coef:].reshape(n_dev * tile_count * listed, 4)

    vband = band_matrix(vert_taps, tile_side)
    hband = band_matrix(horiz_taps, tile_side)

    rows_pass = jnp.einsum("tyk,bxk->tybx", tiles, hband, preferred_element_type=jnp.float32)

    exposures = packed.shape[0]
    picker = (tile_exposure[:, None] == jnp.arange(exposures, dtype=jnp.int32)[None, :]).astype(
        jnp.bfloat16
    )
    picked = jnp.dot(picker, packed, preferred_element_type=jnp.float32)
    coef_tile = picked[:, :terms]
    weight_tile = picked[:, terms]

    partial_value = (rows_pass * coef_tile[:, None, :, None]).astype(jnp.bfloat16)
    smoothed = jnp.einsum(
        "byk,tkbx->tyx", vband, partial_value, preferred_element_type=jnp.float32
    )
    weighted = (weight_tile[:, None, None] * smoothed).astype(jnp.bfloat16)

    e = lax.axis_index(EXP)
    row_entries = n_bands * tile_count * listed
    got_meta = lax.dynamic_slice_in_dim(all_entries, e * row_entries, row_entries, axis=0)
    row_tiles = lax.all_gather(weighted, "grp", axis=0, tiled=True)
    entries = got_meta.shape[0]
    sources = row_tiles.shape[0]
    got_patch = got_meta[:, 0].astype(jnp.int32)
    got_row = got_meta[:, 1].astype(jnp.int32).reshape(sources, listed)
    shape4 = (sources, listed, band_rows, tile_side)
    inner = lax.broadcasted_iota(jnp.int32, shape4, 2)
    src = lax.broadcasted_iota(jnp.int32, shape4, 3)
    picks = (src == g * band_rows + inner - got_row[:, :, None, None]).astype(jnp.bfloat16)
    got_slabs = jnp.einsum("sjiy,syx->sjix", picks, row_tiles, preferred_element_type=jnp.float32)
    got_slabs = got_slabs.astype(jnp.bfloat16).reshape(entries, band_rows, tile_side)
    got_col = got_meta[:, 2].astype(jnp.int32)

    x_in = lax.broadcasted_iota(jnp.int32, (entries, tile_side, PS), 1)
    x_out = lax.broadcasted_iota(jnp.int32, (entries, tile_side, PS), 2)
    shifter = (x_out == got_col[:, None, None] + x_in).astype(jnp.bfloat16)
    shifted = jnp.einsum("kyx,kxX->kyX", got_slabs, shifter, preferred_element_type=jnp.float32)
    shifted = shifted.astype(jnp.bfloat16)
    chips = n_owners // n_halves
    chip_patch = n_halves * jnp.arange(chips, dtype=jnp.int32)[:, None]
    flat_shifted = shifted.reshape(entries, band_rows * PS)
    give_of = (got_patch[None, :] == chip_patch + (1 - h)).astype(jnp.bfloat16)
    give = jnp.einsum("pk,kyX->pyX", give_of, shifted, preferred_element_type=jnp.float32)
    got_give = lax.ppermute(give.astype(jnp.bfloat16), "ec", perm=[(0, 1), (1, 0)])
    keep_of = (got_patch[None, :] == chip_patch + h).astype(jnp.bfloat16)
    keep = jnp.einsum("pk,kyX->pyX", keep_of, shifted, preferred_element_type=jnp.float32)

    pair = (keep + got_give.astype(jnp.float32)).reshape(chips, band_rows, PS)
    recv_bands = lax.all_to_all(pair.astype(jnp.bfloat16), CHIP, split_axis=0, concat_axis=0, tiled=True)
    flux = jnp.sum(recv_bands.astype(jnp.float32), axis=0)
    rows = all_entries[:, 1].astype(jnp.int32)
    cols = all_entries[:, 2].astype(jnp.int32)
    entry_exposure = all_entries[:, 3].astype(jnp.int32)
    exposure_pick = (
        entry_exposure[:, None] == jnp.arange(exposures, dtype=jnp.int32)[None, :]
    ).astype(jnp.bfloat16)
    wts = jnp.dot(exposure_pick, packed[:, terms], preferred_element_type=jnp.float32)
    wts = jnp.where(all_entries[:, 0].astype(jnp.int32) == e, wts, 0.0)
    y_index = g * band_rows + jnp.arange(band_rows, dtype=jnp.int32)
    x_index = jnp.arange(PS, dtype=jnp.int32)
    row_mask = (
        (y_index[None, :] >= rows[:, None]) & (y_index[None, :] < rows[:, None] + tile_side)
    ).astype(jnp.float32) * wts[:, None]
    col_mask = (
        (x_index[None, :] >= cols[:, None]) & (x_index[None, :] < cols[:, None] + tile_side)
    ).astype(jnp.float32)
    cover = jnp.einsum(
        "my,mx->yx",
        row_mask.astype(jnp.bfloat16),
        col_mask.astype(jnp.bfloat16),
        preferred_element_type=jnp.float32,
    )
    cover = lax.optimization_barrier(cover)
    coadd = flux / jnp.maximum(cover, 1.0)
    return coadd[None]


def solution(mesh):
    n_exp, n_grp = mesh.devices.shape
    n_core = 2
    n_y = 4
    split = Mesh(mesh.devices.reshape(n_y, n_exp // (n_y * n_core), n_core, n_grp), EXP + ("grp",))
    every = EXP + ("grp",)
    in_specs = (
        P(every, None, None),
        P(every),
        P(every, None),
        P(every, None, None),
        P(every, None),
        P(every),
        P(),
        P(),
    )
    out_specs = P(EXP, "grp", None)
    return jax.shard_map(
        per_device, mesh=split, in_specs=in_specs, out_specs=out_specs, check_vma=False
    )
```

```python
import jax
import jax.numpy as jnp
from jax import lax
from jax.sharding import Mesh
from jax.sharding import PartitionSpec as P

PS = 512
EXP = ("ey", "ez", "ec")
CHIP = ("ey", "ez")


def band_matrix(filters, tile_side):
    terms, kernel_width = filters.shape
    half_width = (kernel_width - 1) // 2
    row = lax.broadcasted_iota(jnp.int32, (kernel_width, tile_side, tile_side), 1)
    col = lax.broadcasted_iota(jnp.int32, (kernel_width, tile_side, tile_side), 2)
    tap = lax.broadcasted_iota(jnp.int32, (kernel_width, tile_side, tile_side), 0)
    onehot = (col - row + half_width == tap).astype(jnp.bfloat16)
    band = jnp.einsum("bd,dij->bij", filters, onehot, preferred_element_type=jnp.float32)
    return band.astype(jnp.bfloat16)


def per_device(
    tiles, tile_exposure, tile_patch, tile_offset, coeffs, inv_var, vert_taps, horiz_taps
):
    n_owners = lax.axis_size(EXP)
    n_bands = lax.axis_size("grp")
    tile_count, tile_side, _ = tiles.shape
    listed = tile_patch.shape[1]
    terms = coeffs.shape[1]
    band_rows = PS // n_bands
    g = lax.axis_index("grp")
    h = lax.axis_index("ec")
    n_halves = lax.axis_size("ec")

    n_dev = n_owners * n_bands
    packed = jnp.concatenate([coeffs, inv_var[:, None]], axis=1).astype(jnp.float32)
    own_entries = jnp.stack(
        [
            tile_patch,
            tile_offset[:, :, 0],
            tile_offset[:, :, 1],
            jnp.broadcast_to(tile_exposure[:, None], (tile_count, listed)),
        ],
        axis=-1,
    ).astype(jnp.float32)
    payload = jnp.concatenate([packed.reshape(-1), own_entries.reshape(-1)])
    width = payload.shape[0]
    payload = jnp.broadcast_to(payload[None], (n_bands, width))
    payload = lax.all_to_all(payload, "grp", split_axis=0, concat_axis=0, tiled=True)
    payload = jnp.broadcast_to(payload.reshape(1, 1, n_bands * width), (n_owners, 1, n_bands * width))
    payload = lax.all_to_all(payload, EXP, split_axis=0, concat_axis=0, tiled=True)
    payload = payload.reshape(n_dev, width)
    per_dev_coef = packed.size
    packed = payload[:, :per_dev_coef].reshape(-1, terms + 1).astype(jnp.bfloat16)
    all_entries = payload[:, per_dev_coef:].reshape(n_dev * tile_count * listed, 4)

    vband = band_matrix(vert_taps, tile_side)
    hband = band_matrix(horiz_taps, tile_side)

    rows_pass = jnp.einsum("tyk,bxk->tybx", tiles, hband, preferred_element_type=jnp.float32)

    exposures = packed.shape[0]
    picker = (tile_exposure[:, None] == jnp.arange(exposures, dtype=jnp.int32)[None, :]).astype(
        jnp.bfloat16
    )
    picked = jnp.dot(picker, packed, preferred_element_type=jnp.float32)
    coef_tile = picked[:, :terms]
    weight_tile = picked[:, terms]

    partial_value = (rows_pass * coef_tile[:, None, :, None]).astype(jnp.bfloat16)
    smoothed = jnp.einsum(
        "byk,tkbx->tyx", vband, partial_value, preferred_element_type=jnp.float32
    )
    weighted = (weight_tile[:, None, None] * smoothed).astype(jnp.bfloat16)

    e = lax.axis_index(EXP)
    row_entries = n_bands * tile_count * listed
    got_meta = lax.dynamic_slice_in_dim(all_entries, e * row_entries, row_entries, axis=0)
    pieces = [weighted] + [
        lax.ppermute(weighted, "grp", perm=[(i, (i + d) % n_bands) for i in range(n_bands)])
        for d in range(1, n_bands)
    ]
    row_tiles = jnp.concatenate(pieces, axis=0)
    from_peer = (g - jnp.arange(n_bands, dtype=jnp.int32)) % n_bands
    got_meta = jnp.take(got_meta.reshape(n_bands, -1, 4), from_peer, axis=0).reshape(-1, 4)
    entries = got_meta.shape[0]
    sources = row_tiles.shape[0]
    got_patch = got_meta[:, 0].astype(jnp.int32)
    got_row = got_meta[:, 1].astype(jnp.int32).reshape(sources, listed)
    shape4 = (sources, listed, band_rows, tile_side)
    inner = lax.broadcasted_iota(jnp.int32, shape4, 2)
    src = lax.broadcasted_iota(jnp.int32, shape4, 3)
    picks = (src == g * band_rows + inner - got_row[:, :, None, None]).astype(jnp.bfloat16)
    got_slabs = jnp.einsum("sjiy,syx->sjix", picks, row_tiles, preferred_element_type=jnp.float32)
    got_slabs = got_slabs.astype(jnp.bfloat16).reshape(entries, band_rows, tile_side)
    got_col = got_meta[:, 2].astype(jnp.int32)

    x_in = lax.broadcasted_iota(jnp.int32, (entries, tile_side, PS), 1)
    x_out = lax.broadcasted_iota(jnp.int32, (entries, tile_side, PS), 2)
    shifter = (x_out == got_col[:, None, None] + x_in).astype(jnp.bfloat16)
    shifted = jnp.einsum("kyx,kxX->kyX", got_slabs, shifter, preferred_element_type=jnp.float32)
    shifted = shifted.astype(jnp.bfloat16)
    chips = n_owners // n_halves
    chip_patch = n_halves * jnp.arange(chips, dtype=jnp.int32)[:, None]
    flat_shifted = shifted.reshape(entries, band_rows * PS)
    give_of = (got_patch[None, :] == chip_patch + (1 - h)).astype(jnp.bfloat16)
    give = jnp.dot(give_of, flat_shifted, preferred_element_type=jnp.float32)
    got_give = lax.ppermute(give.astype(jnp.bfloat16), "ec", perm=[(0, 1), (1, 0)])
    keep_of = (got_patch[None, :] == chip_patch + h).astype(jnp.bfloat16)
    keep = jnp.dot(keep_of, flat_shifted, preferred_element_type=jnp.float32)

    pair = (keep + got_give.astype(jnp.float32)).reshape(chips, band_rows, PS)
    recv_bands = lax.all_to_all(pair.astype(jnp.bfloat16), CHIP, split_axis=0, concat_axis=0, tiled=True)
    flux = jnp.sum(recv_bands.astype(jnp.float32), axis=0)
    rows = all_entries[:, 1].astype(jnp.int32)
    cols = all_entries[:, 2].astype(jnp.int32)
    entry_exposure = all_entries[:, 3].astype(jnp.int32)
    exposure_pick = (
        entry_exposure[:, None] == jnp.arange(exposures, dtype=jnp.int32)[None, :]
    ).astype(jnp.bfloat16)
    wts = jnp.dot(exposure_pick, packed[:, terms], preferred_element_type=jnp.float32)
    wts = jnp.where(all_entries[:, 0].astype(jnp.int32) == e, wts, 0.0)
    y_index = g * band_rows + jnp.arange(band_rows, dtype=jnp.int32)
    x_index = jnp.arange(PS, dtype=jnp.int32)
    row_mask = (
        (y_index[None, :] >= rows[:, None]) & (y_index[None, :] < rows[:, None] + tile_side)
    ).astype(jnp.float32) * wts[:, None]
    col_mask = (
        (x_index[None, :] >= cols[:, None]) & (x_index[None, :] < cols[:, None] + tile_side)
    ).astype(jnp.float32)
    cover = jnp.einsum(
        "my,mx->yx",
        row_mask.astype(jnp.bfloat16),
        col_mask.astype(jnp.bfloat16),
        preferred_element_type=jnp.float32,
    )
    cover = lax.optimization_barrier(cover)
    coadd = flux / jnp.maximum(cover, 1.0)
    return coadd[None]


def solution(mesh):
    n_exp, n_grp = mesh.devices.shape
    n_core = 2
    n_y = 4
    split = Mesh(mesh.devices.reshape(n_y, n_exp // (n_y * n_core), n_core, n_grp), EXP + ("grp",))
    every = EXP + ("grp",)
    in_specs = (
        P(every, None, None),
        P(every),
        P(every, None),
        P(every, None, None),
        P(every, None),
        P(every),
        P(),
        P(),
    )
    out_specs = P(EXP, "grp", None)
    return jax.shard_map(
        per_device, mesh=split, in_specs=in_specs, out_specs=out_specs, check_vma=False
    )
```

```python
import jax
import jax.numpy as jnp
from jax import lax
from jax.sharding import Mesh
from jax.sharding import PartitionSpec as P

PS = 512
EXP = ("ey", "ez", "ec")
CHIP = ("ey", "ez")


def band_matrix(filters, tile_side):
    terms, kernel_width = filters.shape
    half_width = (kernel_width - 1) // 2
    row = lax.broadcasted_iota(jnp.int32, (kernel_width, tile_side, tile_side), 1)
    col = lax.broadcasted_iota(jnp.int32, (kernel_width, tile_side, tile_side), 2)
    tap = lax.broadcasted_iota(jnp.int32, (kernel_width, tile_side, tile_side), 0)
    onehot = (col - row + half_width == tap).astype(jnp.bfloat16)
    band = jnp.einsum("bd,dij->bij", filters, onehot, preferred_element_type=jnp.float32)
    return band.astype(jnp.bfloat16)


def per_device(
    tiles, tile_exposure, tile_patch, tile_offset, coeffs, inv_var, vert_taps, horiz_taps
):
    n_owners = lax.axis_size(EXP)
    n_bands = lax.axis_size("grp")
    tile_count, tile_side, _ = tiles.shape
    listed = tile_patch.shape[1]
    terms = coeffs.shape[1]
    band_rows = PS // n_bands
    g = lax.axis_index("grp")
    h = lax.axis_index("ec")
    n_halves = lax.axis_size("ec")

    n_dev = n_owners * n_bands
    packed = jnp.concatenate([coeffs, inv_var[:, None]], axis=1).astype(jnp.float32)
    own_entries = jnp.stack(
        [
            tile_patch,
            tile_offset[:, :, 0],
            tile_offset[:, :, 1],
            jnp.broadcast_to(tile_exposure[:, None], (tile_count, listed)),
        ],
        axis=-1,
    ).astype(jnp.float32)
    payload = jnp.concatenate([packed.reshape(-1), own_entries.reshape(-1)])
    width = payload.shape[0]
    payload = jnp.broadcast_to(payload[None], (n_bands, width))
    payload = lax.all_to_all(payload, "grp", split_axis=0, concat_axis=0, tiled=True)
    payload = jnp.broadcast_to(payload.reshape(1, 1, n_bands * width), (n_owners, 1, n_bands * width))
    payload = lax.all_to_all(payload, EXP, split_axis=0, concat_axis=0, tiled=True)
    payload = payload.reshape(n_dev, width)
    per_dev_coef = packed.size
    packed = payload[:, :per_dev_coef].reshape(-1, terms + 1).astype(jnp.bfloat16)
    all_entries = payload[:, per_dev_coef:].reshape(n_dev * tile_count * listed, 4)

    vband = band_matrix(vert_taps, tile_side)
    hband = band_matrix(horiz_taps, tile_side)

    rows_pass = jnp.einsum("tyk,bxk->tybx", tiles, hband, preferred_element_type=jnp.float32)

    exposures = packed.shape[0]
    picker = (tile_exposure[:, None] == jnp.arange(exposures, dtype=jnp.int32)[None, :]).astype(
        jnp.bfloat16
    )
    picked = jnp.dot(picker, packed, preferred_element_type=jnp.float32)
    coef_tile = picked[:, :terms]
    weight_tile = picked[:, terms]

    partial_value = (rows_pass * coef_tile[:, None, :, None]).astype(jnp.bfloat16)
    smoothed = jnp.einsum(
        "byk,tkbx->tyx", vband, partial_value, preferred_element_type=jnp.float32
    )
    weighted = (weight_tile[:, None, None] * smoothed).astype(jnp.bfloat16)

    e = lax.axis_index(EXP)
    row_entries = n_bands * tile_count * listed
    got_meta = lax.dynamic_slice_in_dim(all_entries, e * row_entries, row_entries, axis=0)
    up = [(i, (i + 1) % n_bands) for i in range(n_bands)]
    down = [(i, (i - 1) % n_bands) for i in range(n_bands)]
    from_below = lax.ppermute(weighted, "grp", perm=up)
    from_above = lax.ppermute(weighted, "grp", perm=down)
    half = tile_count // 2
    from_two = jnp.concatenate(
        [
            lax.ppermute(from_below[:half], "grp", perm=up),
            lax.ppermute(from_above[half:], "grp", perm=down),
        ],
        axis=0,
    )
    pieces = [weighted, from_below, from_two, from_above]
    row_tiles = jnp.concatenate(pieces, axis=0)
    from_peer = (g - jnp.arange(n_bands, dtype=jnp.int32)) % n_bands
    got_meta = jnp.take(got_meta.reshape(n_bands, -1, 4), from_peer, axis=0).reshape(-1, 4)
    entries = got_meta.shape[0]
    sources = row_tiles.shape[0]
    got_patch = got_meta[:, 0].astype(jnp.int32)
    got_row = got_meta[:, 1].astype(jnp.int32).reshape(sources, listed)
    shape4 = (sources, listed, band_rows, tile_side)
    inner = lax.broadcasted_iota(jnp.int32, shape4, 2)
    src = lax.broadcasted_iota(jnp.int32, shape4, 3)
    picks = (src == g * band_rows + inner - got_row[:, :, None, None]).astype(jnp.bfloat16)
    got_slabs = jnp.einsum("sjiy,syx->sjix", picks, row_tiles, preferred_element_type=jnp.float32)
    got_slabs = got_slabs.astype(jnp.bfloat16).reshape(entries, band_rows, tile_side)
    got_col = got_meta[:, 2].astype(jnp.int32)

    x_in = lax.broadcasted_iota(jnp.int32, (entries, tile_side, PS), 1)
    x_out = lax.broadcasted_iota(jnp.int32, (entries, tile_side, PS), 2)
    shifter = (x_out == got_col[:, None, None] + x_in).astype(jnp.bfloat16)
    shifted = jnp.einsum("kyx,kxX->kyX", got_slabs, shifter, preferred_element_type=jnp.float32)
    shifted = shifted.astype(jnp.bfloat16)
    chips = n_owners // n_halves
    chip_patch = n_halves * jnp.arange(chips, dtype=jnp.int32)[:, None]
    flat_shifted = shifted.reshape(entries, band_rows * PS)
    give_of = (got_patch[None, :] == chip_patch + (1 - h)).astype(jnp.bfloat16)
    give = jnp.dot(give_of, flat_shifted, preferred_element_type=jnp.float32)
    got_give = lax.ppermute(give.astype(jnp.bfloat16), "ec", perm=[(0, 1), (1, 0)])
    keep_of = (got_patch[None, :] == chip_patch + h).astype(jnp.bfloat16)
    keep = jnp.dot(keep_of, flat_shifted, preferred_element_type=jnp.float32)

    pair = (keep + got_give.astype(jnp.float32)).reshape(chips, band_rows, PS)
    recv_bands = lax.all_to_all(pair.astype(jnp.bfloat16), CHIP, split_axis=0, concat_axis=0, tiled=True)
    flux = jnp.sum(recv_bands.astype(jnp.float32), axis=0)
    rows = all_entries[:, 1].astype(jnp.int32)
    cols = all_entries[:, 2].astype(jnp.int32)
    entry_exposure = all_entries[:, 3].astype(jnp.int32)
    exposure_pick = (
        entry_exposure[:, None] == jnp.arange(exposures, dtype=jnp.int32)[None, :]
    ).astype(jnp.bfloat16)
    wts = jnp.dot(exposure_pick, packed[:, terms], preferred_element_type=jnp.float32)
    wts = jnp.where(all_entries[:, 0].astype(jnp.int32) == e, wts, 0.0)
    y_index = g * band_rows + jnp.arange(band_rows, dtype=jnp.int32)
    x_index = jnp.arange(PS, dtype=jnp.int32)
    row_mask = (
        (y_index[None, :] >= rows[:, None]) & (y_index[None, :] < rows[:, None] + tile_side)
    ).astype(jnp.float32) * wts[:, None]
    col_mask = (
        (x_index[None, :] >= cols[:, None]) & (x_index[None, :] < cols[:, None] + tile_side)
    ).astype(jnp.float32)
    cover = jnp.einsum(
        "my,mx->yx",
        row_mask.astype(jnp.bfloat16),
        col_mask.astype(jnp.bfloat16),
        preferred_element_type=jnp.float32,
    )
    cover = lax.optimization_barrier(cover)
    coadd = flux / jnp.maximum(cover, 1.0)
    return coadd[None]


def solution(mesh):
    n_exp, n_grp = mesh.devices.shape
    n_core = 2
    n_y = 4
    split = Mesh(mesh.devices.reshape(n_y, n_exp // (n_y * n_core), n_core, n_grp), EXP + ("grp",))
    every = EXP + ("grp",)
    in_specs = (
        P(every, None, None),
        P(every),
        P(every, None),
        P(every, None, None),
        P(every, None),
        P(every),
        P(),
        P(),
    )
    out_specs = P(EXP, "grp", None)
    return jax.shard_map(
        per_device, mesh=split, in_specs=in_specs, out_specs=out_specs, check_vma=False
    )
```

```python
import jax
import jax.numpy as jnp
from jax import lax
from jax.sharding import Mesh
from jax.sharding import PartitionSpec as P

PS = 512
EXP = ("ey", "ez", "ec")
CHIP = ("ey", "ez")


def band_matrix(filters, tile_side):
    terms, kernel_width = filters.shape
    half_width = (kernel_width - 1) // 2
    row = lax.broadcasted_iota(jnp.int32, (kernel_width, tile_side, tile_side), 1)
    col = lax.broadcasted_iota(jnp.int32, (kernel_width, tile_side, tile_side), 2)
    tap = lax.broadcasted_iota(jnp.int32, (kernel_width, tile_side, tile_side), 0)
    onehot = (col - row + half_width == tap).astype(jnp.bfloat16)
    band = jnp.einsum("bd,dij->bij", filters, onehot, preferred_element_type=jnp.float32)
    return band.astype(jnp.bfloat16)


def per_device(
    tiles, tile_exposure, tile_patch, tile_offset, coeffs, inv_var, vert_taps, horiz_taps
):
    n_owners = lax.axis_size(EXP)
    n_bands = lax.axis_size("grp")
    tile_count, tile_side, _ = tiles.shape
    listed = tile_patch.shape[1]
    terms = coeffs.shape[1]
    band_rows = PS // n_bands
    g = lax.axis_index("grp")
    h = lax.axis_index("ec")
    n_halves = lax.axis_size("ec")

    n_dev = n_owners * n_bands
    packed = jnp.concatenate([coeffs, inv_var[:, None]], axis=1).astype(jnp.float32)
    own_entries = jnp.stack(
        [
            tile_patch,
            tile_offset[:, :, 0],
            tile_offset[:, :, 1],
            jnp.broadcast_to(tile_exposure[:, None], (tile_count, listed)),
        ],
        axis=-1,
    ).astype(jnp.float32)
    payload = jnp.concatenate([packed.reshape(-1), own_entries.reshape(-1)])
    width = payload.shape[0]
    payload = jnp.broadcast_to(payload[None], (n_bands, width))
    payload = lax.all_to_all(payload, "grp", split_axis=0, concat_axis=0, tiled=True)
    payload = jnp.broadcast_to(payload.reshape(1, 1, n_bands * width), (n_owners, 1, n_bands * width))
    payload = lax.all_to_all(payload, EXP, split_axis=0, concat_axis=0, tiled=True)
    payload = payload.reshape(n_dev, width)
    per_dev_coef = packed.size
    packed = payload[:, :per_dev_coef].reshape(-1, terms + 1).astype(jnp.bfloat16)
    all_entries = payload[:, per_dev_coef:].reshape(n_dev * tile_count * listed, 4)

    vband = band_matrix(vert_taps, tile_side)
    hband = band_matrix(horiz_taps, tile_side)

    rows_pass = jnp.einsum("tyk,bxk->tybx", tiles, hband, preferred_element_type=jnp.float32)

    exposures = packed.shape[0]
    picker = (tile_exposure[:, None] == jnp.arange(exposures, dtype=jnp.int32)[None, :]).astype(
        jnp.bfloat16
    )
    picked = jnp.dot(picker, packed, preferred_element_type=jnp.float32)
    coef_tile = picked[:, :terms]
    weight_tile = picked[:, terms]

    partial_value = (rows_pass * coef_tile[:, None, :, None]).astype(jnp.bfloat16)
    smoothed = jnp.einsum(
        "byk,tkbx->tyx", vband, partial_value, preferred_element_type=jnp.float32
    )
    weighted = (weight_tile[:, None, None] * smoothed).astype(jnp.bfloat16)

    e = lax.axis_index(EXP)
    row_entries = n_bands * tile_count * listed
    got_meta = lax.dynamic_slice_in_dim(all_entries, e * row_entries, row_entries, axis=0)
    pieces = [weighted] + [
        lax.ppermute(weighted, "grp", perm=[(i, (i + d) % n_bands) for i in range(n_bands)])
        for d in range(1, n_bands)
    ]
    row_tiles = jnp.concatenate(pieces, axis=0)
    from_peer = (g - jnp.arange(n_bands, dtype=jnp.int32)) % n_bands
    got_meta = jnp.take(got_meta.reshape(n_bands, -1, 4), from_peer, axis=0).reshape(-1, 4)
    entries = got_meta.shape[0]
    sources = row_tiles.shape[0]
    got_patch = got_meta[:, 0].astype(jnp.int32)
    got_row = got_meta[:, 1].astype(jnp.int32).reshape(sources, listed)
    shape4 = (sources, listed, band_rows, tile_side)
    inner = lax.broadcasted_iota(jnp.int32, shape4, 2)
    src = lax.broadcasted_iota(jnp.int32, shape4, 3)
    picks = (src == g * band_rows + inner - got_row[:, :, None, None]).astype(jnp.bfloat16)
    got_slabs = jnp.einsum("sjiy,syx->sjix", picks, row_tiles, preferred_element_type=jnp.float32)
    got_slabs = got_slabs.astype(jnp.bfloat16).reshape(entries, band_rows, tile_side)
    got_col = got_meta[:, 2].astype(jnp.int32)

    x_in = lax.broadcasted_iota(jnp.int32, (entries, tile_side, PS), 1)
    x_out = lax.broadcasted_iota(jnp.int32, (entries, tile_side, PS), 2)
    shifter = (x_out == got_col[:, None, None] + x_in).astype(jnp.bfloat16)
    shifted = jnp.einsum("kyx,kxX->kyX", got_slabs, shifter, preferred_element_type=jnp.float32)
    shifted = shifted.astype(jnp.bfloat16)
    chips = n_owners // n_halves
    chip_patch = n_halves * jnp.arange(chips, dtype=jnp.int32)[:, None]
    flat_shifted = shifted.reshape(entries, band_rows * PS)
    give_of = (got_patch[None, :] == chip_patch + (1 - h)).astype(jnp.bfloat16)
    split_at = chips // 2
    got_give = jnp.concatenate(
        [
            lax.ppermute(
                jnp.dot(part, flat_shifted, preferred_element_type=jnp.float32).astype(
                    jnp.bfloat16
                ),
                "ec",
                perm=[(0, 1), (1, 0)],
            )
            for part in (give_of[:split_at], give_of[split_at:])
        ],
        axis=0,
    )
    keep_of = (got_patch[None, :] == chip_patch + h).astype(jnp.bfloat16)
    keep = jnp.dot(keep_of, flat_shifted, preferred_element_type=jnp.float32)

    pair = (keep + got_give.astype(jnp.float32)).reshape(chips, band_rows, PS)
    recv_bands = lax.all_to_all(pair.astype(jnp.bfloat16), CHIP, split_axis=0, concat_axis=0, tiled=True)
    flux = jnp.sum(recv_bands.astype(jnp.float32), axis=0)
    rows = all_entries[:, 1].astype(jnp.int32)
    cols = all_entries[:, 2].astype(jnp.int32)
    entry_exposure = all_entries[:, 3].astype(jnp.int32)
    exposure_pick = (
        entry_exposure[:, None] == jnp.arange(exposures, dtype=jnp.int32)[None, :]
    ).astype(jnp.bfloat16)
    wts = jnp.dot(exposure_pick, packed[:, terms], preferred_element_type=jnp.float32)
    wts = jnp.where(all_entries[:, 0].astype(jnp.int32) == e, wts, 0.0)
    y_index = g * band_rows + jnp.arange(band_rows, dtype=jnp.int32)
    x_index = jnp.arange(PS, dtype=jnp.int32)
    row_mask = (
        (y_index[None, :] >= rows[:, None]) & (y_index[None, :] < rows[:, None] + tile_side)
    ).astype(jnp.float32) * wts[:, None]
    col_mask = (
        (x_index[None, :] >= cols[:, None]) & (x_index[None, :] < cols[:, None] + tile_side)
    ).astype(jnp.float32)
    cover = jnp.einsum(
        "my,mx->yx",
        row_mask.astype(jnp.bfloat16),
        col_mask.astype(jnp.bfloat16),
        preferred_element_type=jnp.float32,
    )
    cover = lax.optimization_barrier(cover)
    coadd = flux / jnp.maximum(cover, 1.0)
    return coadd[None]


def solution(mesh):
    n_exp, n_grp = mesh.devices.shape
    n_core = 2
    n_y = 4
    split = Mesh(mesh.devices.reshape(n_y, n_exp // (n_y * n_core), n_core, n_grp), EXP + ("grp",))
    every = EXP + ("grp",)
    in_specs = (
        P(every, None, None),
        P(every),
        P(every, None),
        P(every, None, None),
        P(every, None),
        P(every),
        P(),
        P(),
    )
    out_specs = P(EXP, "grp", None)
    return jax.shard_map(
        per_device, mesh=split, in_specs=in_specs, out_specs=out_specs, check_vma=False
    )
```
